256 devices in a mesh: section: 2 (over core), dp: 16 (over y_hi, z), cls: 8 (over x, y_lo).
Axes of the slice: x: 4, y: 4 (y_hi: 2, y_lo: 2; y = y_hi * 2 + y_lo), z: 8, core: 2. Of those that a mesh axis runs over, the one named last changes fastest.
Arguments:
- embeddings: bfloat16 [2048, 512], P('dp')
- centers: bfloat16 [1048576, 512], P(('section', 'dp', 'cls'))
- sample_ids: int32 [256, 1536], P(('section', 'dp', 'cls')), may hold values from 0 to 4095, as said below
- labels: int32 [2048], P('dp'), may hold values from 0 to 1048575, as said below
Outputs:
- feature_grad: float32 [2048, 512], P(('section', 'dp', 'cls'))
- row_loss: float32 [2048], P('dp')
The draws below stay inside these ranges and needn't reach their ends.
Inputs may be any that keep to these rules, and one draw needn't show every extreme that they name: `sample_ids`: the 1536 entries of each row are distinct. For each row, labels // 4096 names a shard j, and labels % 4096 is among sample_ids[j].
All inputs are finite; a program needn't handle non-finite values.
Results may differ from the reference program's by a relative error of at most 0.0033.
Values may be sent and summed in bfloat16 or wider, within the bound.
No kernel may reach another device: no remote copies, remote signals or barrier semaphores. Data moves between devices by JAX's collectives and lax.ppermute only.
A program may use at most 64 MiB of HBM per device.

```python
import jax
import jax.numpy as jnp
from jax import lax

D = 512
CLS_DEV = 4096
K = 1536
SHARDS = 256
CLASSES = 1048576
ROWS = 2048


def shard_orders(key):
    keys = jax.random.split(jax.random.fold_in(key, 7), SHARDS)
    return jax.vmap(lambda one_key: jax.random.permutation(one_key, CLS_DEV))(keys).astype(jnp.int32)


def draw_sample_ids(key, part):
    orders = shard_orders(key)
    return orders[:, :K].astype(jnp.int32)


def draw_labels(key, part):
    orders = shard_orders(key)
    shard_pick = jax.random.randint(jax.random.fold_in(key, 11), (ROWS,), 0, SHARDS)
    slot_pick = jax.random.randint(jax.random.fold_in(key, 13), (ROWS,), 0, K // 2)
    inside = orders[shard_pick, slot_pick]
    return (shard_pick * CLS_DEV + inside).astype(jnp.int32)


def draw_embeddings(key, part):
    first_key = jax.random.fold_in(key, 21)
    second_key = jax.random.fold_in(key, 22)
    base = jax.random.normal(first_key, (ROWS, D), jnp.float32)
    scales = jnp.exp(jax.random.uniform(second_key, (ROWS, 1), jnp.float32, jnp.log(0.3), jnp.log(3.0)))
    return (base * scales / jnp.sqrt(jnp.float32(D))).astype(jnp.bfloat16)


def draw_centers(key, part):
    first_key = jax.random.fold_in(key, 31)
    second_key = jax.random.fold_in(key, 32)
    base = jax.random.normal(first_key, (CLASSES, D), jnp.float32)
    scales = jnp.exp(jax.random.uniform(second_key, (CLASSES, 1), jnp.float32, 0.0, jnp.log(10.0)))
    return (base * scales / jnp.sqrt(jnp.float32(D))).astype(jnp.bfloat16)


def setup_inputs(seed: int = 0) -> dict:
    key_of = jax.random.split(jax.random.key(seed), 5)
    embeddings = draw_embeddings(jax.random.fold_in(key_of[4], 71), 0)
    centers = draw_centers(jax.random.fold_in(key_of[4], 71), 0)
    sample_ids = draw_sample_ids(jax.random.fold_in(key_of[4], 71), 0)
    labels = draw_labels(jax.random.fold_in(key_of[4], 71), 0)
    return dict(embeddings=embeddings, centers=centers, sample_ids=sample_ids, labels=labels)


LOGIT_SCALE = 64.0
MARGIN = 0.35
EPSILON = 1e-06

def reference(embeddings, centers, sample_ids, labels):
    shard_count = sample_ids.shape[0]
    width = embeddings.shape[1]
    row_count = embeddings.shape[0]
    emb_float = embeddings.astype(jnp.float32)
    row_norm = jnp.sqrt(lax.optimization_barrier(jnp.sum(emb_float * emb_float, axis=1)) + EPSILON)
    unit_rows = (emb_float / row_norm[:, None]).astype(jnp.bfloat16)
    center_blocks = centers.reshape(shard_count, CLS_DEV, width)
    shard_numbers = jnp.arange(shard_count, dtype=jnp.int32)

    def one_shard(carry, inputs):
        total, target, unscaled, own = carry
        block, ids, number = inputs
        global_ids = (ids + number * CLS_DEV).astype(jnp.int32)
        chosen = jnp.take(block, ids, axis=0).astype(jnp.float32)
        center_norm = jnp.sqrt(lax.optimization_barrier(jnp.sum(chosen * chosen, axis=1)) + EPSILON)
        unit_centers = (chosen / center_norm[:, None]).astype(jnp.bfloat16)
        cosine = jnp.dot(unit_rows, unit_centers.T, preferred_element_type=jnp.float32)
        matches = global_ids[None, :] == labels[:, None]
        logits = LOGIT_SCALE * cosine - LOGIT_SCALE * MARGIN * matches.astype(cosine.dtype)
        exponent = jnp.exp(logits)
        total = total + lax.optimization_barrier(jnp.sum(exponent, axis=1))
        target = target + lax.optimization_barrier(jnp.sum(jnp.where(matches, logits, jnp.zeros_like(logits)), axis=1))
        weights = exponent.astype(jnp.bfloat16)
        unscaled = unscaled + jnp.dot(weights, unit_centers, preferred_element_type=jnp.float32)
        own = own + jnp.dot(matches.astype(jnp.bfloat16), unit_centers, preferred_element_type=jnp.float32)
        return ((total, target, unscaled, own), None)
    start = (jnp.zeros((row_count,), jnp.float32), jnp.zeros((row_count,), jnp.float32), jnp.zeros((row_count, width), jnp.float32), jnp.zeros((row_count, width), jnp.float32))
    (total, target, unscaled, own_center), _ = lax.scan(one_shard, start, (center_blocks, sample_ids, shard_numbers))
    row_loss = jnp.log(total) - target
    unit_grad = LOGIT_SCALE * (unscaled / total[:, None] - own_center)
    unit_float = emb_float / row_norm[:, None]
    along = lax.optimization_barrier(jnp.sum(unit_float * unit_grad, axis=1, keepdims=True))
    feature_grad = (unit_grad - unit_float * along) / row_norm[:, None]
    return (feature_grad, row_loss)
```

```python
import jax
import jax.numpy as jnp
from jax import lax
from jax.sharding import PartitionSpec as P

LOGIT_SCALE = 64.0
MARGIN = 0.35
EPSILON = 1e-06


def on_device(embeddings, centers, sample_ids, labels):
    shard_index = lax.axis_index(("section", "dp", "cls"))
    per_shard = centers.shape[0]
    gathered, label_all = (
        lax.all_gather(embeddings, "dp", axis=0, tiled=True),
        lax.all_gather(labels, "dp", axis=0, tiled=True),
    )
    total_rows = gathered.shape[0]
    emb_float = gathered.astype(jnp.float32)
    row_norm = jnp.sqrt(jnp.sum(emb_float * emb_float, axis=1) + EPSILON)
    unit_rows = (emb_float / row_norm[:, None]).astype(jnp.bfloat16)
    local_ids = sample_ids[0]
    chosen = jnp.take(centers, local_ids, axis=0).astype(jnp.float32)
    center_norm = jnp.sqrt(jnp.sum(chosen * chosen, axis=1) + EPSILON)
    unit_centers = (chosen / center_norm[:, None]).astype(jnp.bfloat16)
    cosine = lax.dot_general(
        unit_rows, unit_centers, (((1,), (1,)), ((), ())), preferred_element_type=jnp.float32
    )
    local_labels = label_all - shard_index * per_shard
    matches = local_ids[None, :] == local_labels[:, None]
    logits = LOGIT_SCALE * cosine - LOGIT_SCALE * MARGIN * matches.astype(jnp.float32)
    exponent = jnp.exp(logits)
    total_part = jnp.sum(exponent, axis=1)
    target_part = jnp.sum(jnp.where(matches, logits, jnp.float32(0.0)), axis=1)
    total, target = (total_part, target_part)
    for axis in ("section", "cls", "dp"):
        total, target = lax.psum((total, target), axis)
    weights = exponent.astype(jnp.bfloat16)
    column_ids = jnp.arange(local_ids.shape[0], dtype=jnp.int32)
    position = jnp.sum(jnp.where(matches, column_ids[None, :], 0), axis=1)
    owned = jnp.any(matches, axis=1).astype(jnp.float32)
    own_center = jnp.take(unit_centers, position, axis=0).astype(jnp.float32) * owned[:, None]
    section_count = lax.axis_size("section")
    batch_count = lax.axis_size("dp")
    class_count = lax.axis_size("cls")
    rows_here = total_rows // (section_count * batch_count * class_count)
    unscaled = jnp.dot(weights, unit_centers, preferred_element_type=jnp.float32)
    partial = LOGIT_SCALE * (unscaled / total[:, None] - own_center)
    partial = partial.reshape(section_count, batch_count, class_count, rows_here, partial.shape[-1])
    for axis in ("section", "dp", "cls"):
        partial = lax.psum_scatter(partial, axis, scatter_dimension=0, tiled=False)
    unit_grad = partial
    emb_rows = lax.dynamic_slice_in_dim(emb_float, shard_index * rows_here, rows_here, 0)
    norm_rows = lax.dynamic_slice_in_dim(row_norm, shard_index * rows_here, rows_here, 0)
    unit_float = emb_rows / norm_rows[:, None]
    along = jnp.sum(unit_float * unit_grad, axis=1, keepdims=True)
    feature_grad = (unit_grad - unit_float * along) / norm_rows[:, None]
    loss_all = jnp.log(total) - target
    own_rows = embeddings.shape[0]
    row_loss = lax.dynamic_slice_in_dim(loss_all, lax.axis_index("dp") * own_rows, own_rows, 0)
    return (feature_grad, row_loss)


def solution(mesh):
    return jax.shard_map(
        on_device,
        mesh=mesh,
        in_specs=(
            P("dp", None),
            P(("section", "dp", "cls"), None),
            P(("section", "dp", "cls"), None),
            P("dp"),
        ),
        out_specs=(P(("section", "dp", "cls"), None), P("dp")),
        check_vma=False,
    )
```

```python
import jax
import jax.numpy as jnp
from jax import lax
from jax.sharding import PartitionSpec as P

LOGIT_SCALE = 64.0
MARGIN = 0.35
EPSILON = 1e-06
EXTRA = 128


def reduce_chain(payload, section_count, batch_count, class_count):
    rows_here, width = payload.shape[1], payload.shape[2]
    blocks = payload.reshape(section_count, batch_count, class_count, rows_here, width)
    blocks = blocks.transpose(0, 2, 1, 3, 4)
    blocks = lax.all_to_all(blocks, "section", 0, 0, tiled=False).sum(0)
    blocks = lax.all_to_all(blocks, "cls", 0, 0, tiled=False).sum(0)
    blocks = lax.all_to_all(blocks, "dp", 0, 0, tiled=False).sum(0)
    return blocks


def on_device(embeddings, centers, sample_ids, labels):
    shard_index = lax.axis_index(("section", "dp", "cls"))
    per_shard = centers.shape[0]
    gathered, label_all = (
        lax.all_gather(embeddings, "dp", axis=0, tiled=True),
        lax.all_gather(labels, "dp", axis=0, tiled=True),
    )
    total_rows = gathered.shape[0]
    width = gathered.shape[1]
    emb_float = gathered.astype(jnp.float32)
    row_norm = jnp.sqrt(jnp.sum(emb_float * emb_float, axis=1) + EPSILON)
    unit_rows = (emb_float / row_norm[:, None]).astype(jnp.bfloat16)
    local_ids = sample_ids[0]
    chosen = jnp.take(centers, local_ids, axis=0).astype(jnp.float32)
    center_norm = jnp.sqrt(jnp.sum(chosen * chosen, axis=1) + EPSILON)
    unit_centers = (chosen / center_norm[:, None]).astype(jnp.bfloat16)
    cosine = lax.dot_general(
        unit_rows, unit_centers, (((1,), (1,)), ((), ())), preferred_element_type=jnp.float32
    )
    local_labels = label_all - shard_index * per_shard
    matches = local_ids[None, :] == local_labels[:, None]
    logits = LOGIT_SCALE * cosine - LOGIT_SCALE * MARGIN * matches.astype(jnp.float32)
    exponent = jnp.exp(logits)
    total_part = jnp.sum(exponent, axis=1)
    target_part = jnp.sum(jnp.where(matches, logits, jnp.float32(0.0)), axis=1)
    weights = exponent.astype(jnp.bfloat16)
    column_ids = jnp.arange(local_ids.shape[0], dtype=jnp.int32)
    position = jnp.sum(jnp.where(matches, column_ids[None, :], 0), axis=1)
    owned = jnp.any(matches, axis=1).astype(jnp.float32)
    own_center = jnp.take(unit_centers, position, axis=0).astype(jnp.float32) * owned[:, None]
    section_count = lax.axis_size("section")
    batch_count = lax.axis_size("dp")
    class_count = lax.axis_size("cls")
    devices = section_count * batch_count * class_count
    rows_here = total_rows // devices
    rows_per_batch = total_rows // batch_count
    assert rows_here >= 3 and rows_per_batch <= EXTRA and rows_here <= EXTRA
    unscaled = jnp.dot(weights, unit_centers, preferred_element_type=jnp.float32)

    def block_of(values):
        per_batch = values.reshape(batch_count, rows_per_batch)
        per_batch = jnp.pad(per_batch, ((0, 0), (0, EXTRA - rows_per_batch)))
        spread = jnp.broadcast_to(
            per_batch[None, :, None, :], (section_count, batch_count, class_count, EXTRA)
        )
        return spread.reshape(devices, 1, EXTRA)

    own_totals = jnp.pad(total_part.reshape(devices, 1, rows_here), ((0, 0), (0, 0), (0, EXTRA - rows_here)))
    extra = jnp.concatenate(
        [
            block_of(total_part),
            block_of(target_part),
            own_totals,
            jnp.zeros((devices, rows_here - 3, EXTRA), jnp.float32),
        ],
        axis=1,
    )
    payload = jnp.concatenate(
        [
            unscaled.reshape(devices, rows_here, width),
            own_center.reshape(devices, rows_here, width),
            extra,
        ],
        axis=2,
    )
    summed = reduce_chain(payload, section_count, batch_count, class_count)
    unscaled_rows = summed[:, :width]
    own_rows = summed[:, width : 2 * width]
    total_rows_here = summed[2, 2 * width : 2 * width + rows_here]
    unit_grad = LOGIT_SCALE * (unscaled_rows / total_rows_here[:, None] - own_rows)
    emb_rows = lax.dynamic_slice_in_dim(emb_float, shard_index * rows_here, rows_here, 0)
    norm_rows = lax.dynamic_slice_in_dim(row_norm, shard_index * rows_here, rows_here, 0)
    unit_float = emb_rows / norm_rows[:, None]
    along = jnp.sum(unit_float * unit_grad, axis=1, keepdims=True)
    feature_grad = (unit_grad - unit_float * along) / norm_rows[:, None]
    batch_total = summed[0, 2 * width : 2 * width + rows_per_batch]
    batch_target = summed[1, 2 * width : 2 * width + rows_per_batch]
    row_loss = jnp.log(batch_total) - batch_target
    return (feature_grad, row_loss)


def solution(mesh):
    return jax.shard_map(
        on_device,
        mesh=mesh,
        in_specs=(
            P("dp", None),
            P(("section", "dp", "cls"), None),
            P(("section", "dp", "cls"), None),
            P("dp"),
        ),
        out_specs=(P(("section", "dp", "cls"), None), P("dp")),
        check_vma=False,
    )
```

```python
import jax
import jax.numpy as jnp
from jax import lax
from jax.sharding import PartitionSpec as P

LOGIT_SCALE = 64.0
MARGIN = 0.35
EPSILON = 1e-06
EXTRA = 128


def on_device(embeddings, centers, sample_ids, labels):
    section_count = lax.axis_size("section")
    batch_count = lax.axis_size("dp")
    class_count = lax.axis_size("cls")
    assert section_count == 2
    section = lax.axis_index("section")
    batch = lax.axis_index("dp")
    shard_index = lax.axis_index(("section", "dp", "cls"))
    swap = [(0, 1), (1, 0)]
    per_shard = centers.shape[0]
    width = embeddings.shape[1]

    gathered = lax.all_gather(embeddings, "dp", axis=0, tiled=True)
    label_all = lax.all_to_all(
        jnp.broadcast_to(labels[None], (batch_count,) + labels.shape), "dp", 0, 0, tiled=False
    ).reshape(-1)
    total_rows = gathered.shape[0]
    devices = section_count * batch_count * class_count
    rows_here = total_rows // devices
    rows_section = total_rows // section_count
    rows_per_batch = total_rows // batch_count
    batches_per_section = batch_count // section_count
    assert rows_here >= 3 and rows_per_batch <= EXTRA and rows_here <= EXTRA

    local_ids = sample_ids[0]
    chosen = jnp.take(centers, local_ids, axis=0).astype(jnp.float32)
    center_norm = jnp.sqrt(jnp.sum(chosen * chosen, axis=1) + EPSILON)
    unit_centers = (chosen / center_norm[:, None]).astype(jnp.bfloat16)
    global_ids = local_ids + shard_index * per_shard
    partner_centers = lax.ppermute(unit_centers, "section", swap)
    partner_ids = lax.ppermute(global_ids, "section", swap)
    both_centers = jnp.concatenate([unit_centers, partner_centers], axis=0)
    both_ids = jnp.concatenate([global_ids, partner_ids], axis=0)

    section_rows = lax.dynamic_slice_in_dim(gathered, section * rows_section, rows_section, 0)
    section_labels = lax.dynamic_slice_in_dim(label_all, section * rows_section, rows_section, 0)
    emb_float = section_rows.astype(jnp.float32)
    row_norm = jnp.sqrt(jnp.sum(emb_float * emb_float, axis=1) + EPSILON)
    unit_rows = (emb_float / row_norm[:, None]).astype(jnp.bfloat16)

    cosine = lax.dot_general(
        unit_rows, both_centers, (((1,), (1,)), ((), ())), preferred_element_type=jnp.float32
    )
    matches = both_ids[None, :] == section_labels[:, None]
    logits = LOGIT_SCALE * cosine - LOGIT_SCALE * MARGIN * matches.astype(jnp.float32)
    exponent = jnp.exp(logits)
    total_part = jnp.sum(exponent, axis=1)
    target_part = jnp.sum(jnp.where(matches, logits, jnp.float32(0.0)), axis=1)
    weights = exponent.astype(jnp.bfloat16)
    unscaled = jnp.dot(weights, both_centers, preferred_element_type=jnp.float32)
    own_center = jnp.dot(matches.astype(jnp.bfloat16), both_centers, preferred_element_type=jnp.float32)

    def block_of(values):
        blocks = values.reshape(1, batches_per_section, rows_per_batch)
        mine = jnp.arange(section_count, dtype=jnp.int32)[:, None, None] == section
        blocks = jnp.where(mine, blocks, jnp.float32(0.0)).reshape(batch_count, rows_per_batch)
        blocks = jnp.pad(blocks, ((0, 0), (0, EXTRA - rows_per_batch)))
        spread = jnp.broadcast_to(blocks[:, None, :], (batch_count, class_count, EXTRA))
        return spread.reshape(batch_count * class_count, 1, EXTRA)

    dests = batch_count * class_count
    own_totals = jnp.pad(total_part.reshape(dests, 1, rows_here), ((0, 0), (0, 0), (0, EXTRA - rows_here)))
    extra = jnp.concatenate(
        [
            block_of(total_part),
            block_of(target_part),
            own_totals,
            jnp.zeros((dests, rows_here - 3, EXTRA), jnp.float32),
        ],
        axis=1,
    )
    payload = jnp.concatenate(
        [unscaled.reshape(dests, rows_here, width), own_center.reshape(dests, rows_here, width), extra],
        axis=2,
    )
    payload = payload.reshape(batch_count, class_count, rows_here, payload.shape[-1]).transpose(1, 0, 2, 3)
    payload = lax.all_to_all(payload, "cls", 0, 0, tiled=False).sum(0)
    summed = lax.all_to_all(payload, "dp", 0, 0, tiled=False).sum(0)

    block_total = summed[0, 2 * width : 2 * width + rows_per_batch]
    block_target = summed[1, 2 * width : 2 * width + rows_per_batch]
    other_total, other_target = lax.ppermute((block_total, block_target), "section", swap)
    have = batch // batches_per_section == section
    block_total = jnp.where(have, block_total, other_total)
    block_target = jnp.where(have, block_target, other_target)
    row_loss = jnp.log(block_total) - block_target

    unscaled_rows = summed[:, :width]
    own_rows = summed[:, width : 2 * width]
    totals_here = summed[2, 2 * width : 2 * width + rows_here]
    unit_grad = LOGIT_SCALE * (unscaled_rows / totals_here[:, None] - own_rows)
    offset = (shard_index % dests) * rows_here
    emb_rows = lax.dynamic_slice_in_dim(emb_float, offset, rows_here, 0)
    norm_rows = lax.dynamic_slice_in_dim(row_norm, offset, rows_here, 0)
    unit_float = emb_rows / norm_rows[:, None]
    along = jnp.sum(unit_float * unit_grad, axis=1, keepdims=True)
    feature_grad = (unit_grad - unit_float * along) / norm_rows[:, None]
    return (feature_grad, row_loss)


def solution(mesh):
    return jax.shard_map(
        on_device,
        mesh=mesh,
        in_specs=(
            P("dp", None),
            P(("section", "dp", "cls"), None),
            P(("section", "dp", "cls"), None),
            P("dp"),
        ),
        out_specs=(P(("section", "dp", "cls"), None), P("dp")),
        check_vma=False,
    )
```

```python
import jax
import jax.numpy as jnp
from jax import lax
from jax.sharding import PartitionSpec as P

LOGIT_SCALE = 64.0
MARGIN = 0.35
EPSILON = 1e-06
EXTRA = 128


def on_device(embeddings, centers, sample_ids, labels):
    section_count = lax.axis_size("section")
    batch_count = lax.axis_size("dp")
    class_count = lax.axis_size("cls")
    assert section_count == 2 and batch_count % 2 == 0
    section = lax.axis_index("section")
    batch = lax.axis_index("dp")
    cls = lax.axis_index("cls")
    shard_index = lax.axis_index(("section", "dp", "cls"))
    swap = [(0, 1), (1, 0)]
    per_shard = centers.shape[0]
    width = embeddings.shape[1]
    rows_per_batch = embeddings.shape[0]
    half = rows_per_batch // section_count
    devices = section_count * batch_count * class_count
    rows_here = rows_per_batch * batch_count // devices
    assert half == class_count * rows_here and rows_here >= 3 and half <= EXTRA and rows_here <= EXTRA

    my_rows = lax.dynamic_slice_in_dim(embeddings, section * half, half, 0)
    my_labels = lax.dynamic_slice_in_dim(labels, section * half, half, 0)
    gathered = lax.all_gather(my_rows, "dp", axis=0, tiled=True)
    label_all = lax.all_to_all(
        jnp.broadcast_to(my_labels[None], (batch_count,) + my_labels.shape), "dp", 0, 0, tiled=False
    ).reshape(-1)

    local_ids = sample_ids[0]
    chosen = jnp.take(centers, local_ids, axis=0).astype(jnp.float32)
    center_norm = jnp.sqrt(jnp.sum(chosen * chosen, axis=1) + EPSILON)
    unit_centers = (chosen / center_norm[:, None]).astype(jnp.bfloat16)
    global_ids = local_ids + shard_index * per_shard
    partner_centers = lax.ppermute(unit_centers, "section", swap)
    partner_ids = lax.ppermute(global_ids, "section", swap)
    both_centers = jnp.concatenate([unit_centers, partner_centers], axis=0)
    both_ids = jnp.concatenate([global_ids, partner_ids], axis=0)

    emb_float = gathered.astype(jnp.float32)
    row_norm = jnp.sqrt(jnp.sum(emb_float * emb_float, axis=1) + EPSILON)
    unit_rows = (emb_float / row_norm[:, None]).astype(jnp.bfloat16)
    cosine = lax.dot_general(
        unit_rows, both_centers, (((1,), (1,)), ((), ())), preferred_element_type=jnp.float32
    )
    matches = both_ids[None, :] == label_all[:, None]
    logits = LOGIT_SCALE * cosine - LOGIT_SCALE * MARGIN * matches.astype(jnp.float32)
    exponent = jnp.exp(logits)
    total_part = jnp.sum(exponent, axis=1)
    target_part = jnp.sum(jnp.where(matches, logits, jnp.float32(0.0)), axis=1)
    weights = exponent.astype(jnp.bfloat16)
    unscaled = jnp.dot(weights, both_centers, preferred_element_type=jnp.float32)
    own_center = jnp.dot(matches.astype(jnp.bfloat16), both_centers, preferred_element_type=jnp.float32)

    h = batch_count // 2

    def to_dest(values):
        tail = values.shape[1:]
        values = values.reshape((2, h, class_count, rows_here) + tail)
        values = jnp.moveaxis(values, 2, 0)
        values = jnp.swapaxes(values, 1, 2)
        return values.reshape((class_count, batch_count, rows_here) + tail)

    def pad(values):
        return jnp.pad(values, [(0, 0)] * (values.ndim - 1) + [(0, EXTRA - values.shape[-1])])

    block_rows = jnp.broadcast_to(
        jnp.stack([pad(total_part.reshape(batch_count, half)), pad(target_part.reshape(batch_count, half))], axis=1)[None],
        (class_count, batch_count, 2, EXTRA),
    )
    own_totals = pad(to_dest(total_part))[:, :, None, :]
    extra = jnp.concatenate(
        [block_rows, own_totals, jnp.zeros((class_count, batch_count, rows_here - 3, EXTRA), jnp.float32)], axis=2
    )
    payload = jnp.concatenate([to_dest(unscaled), to_dest(own_center), extra], axis=3)
    payload = lax.all_to_all(payload, "cls", 0, 0, tiled=False).sum(0)
    summed = lax.all_to_all(payload, "dp", 0, 0, tiled=False).sum(0)

    half_total = summed[0, 2 * width : 2 * width + half]
    half_target = summed[1, 2 * width : 2 * width + half]
    other_total, other_target = lax.ppermute((half_total, half_target), "section", swap)
    first = section == 0
    block_total = jnp.where(first, jnp.concatenate([half_total, other_total]), jnp.concatenate([other_total, half_total]))
    block_target = jnp.where(first, jnp.concatenate([half_target, other_target]), jnp.concatenate([other_target, half_target]))
    row_loss = jnp.log(block_total) - block_target

    unscaled_rows = summed[:, :width]
    own_rows = summed[:, width : 2 * width]
    totals_here = summed[2, 2 * width : 2 * width + rows_here]
    unit_grad = LOGIT_SCALE * (unscaled_rows / totals_here[:, None] - own_rows)
    source_batch = (batch % 2) * h + batch // 2
    offset = source_batch * half + cls * rows_here
    emb_rows = lax.dynamic_slice_in_dim(emb_float, offset, rows_here, 0)
    norm_rows = lax.dynamic_slice_in_dim(row_norm, offset, rows_here, 0)
    unit_float = emb_rows / norm_rows[:, None]
    along = jnp.sum(unit_float * unit_grad, axis=1, keepdims=True)
    computed = (unit_grad - unit_float * along) / norm_rows[:, None]

    pairs = [
        (s * batch_count + e, (1 - s) * batch_count + (e ^ 1))
        for s in range(2)
        for e in range(batch_count)
        if e % 2 != s
    ]
    received = lax.ppermute(computed, ("section", "dp"), pairs)
    feature_grad = jnp.where(batch % 2 == section, computed, received)
    return (feature_grad, row_loss)


def solution(mesh):
    return jax.shard_map(
        on_device,
        mesh=mesh,
        in_specs=(
            P("dp", None),
            P(("section", "dp", "cls"), None),
            P(("section", "dp", "cls"), None),
            P("dp"),
        ),
        out_specs=(P(("section", "dp", "cls"), None), P("dp")),
        check_vma=False,
    )
```

```python
import jax
import jax.numpy as jnp
from jax import lax
from jax.sharding import PartitionSpec as P

LOGIT_SCALE = 64.0
MARGIN = 0.35
EPSILON = 1e-06
EXTRA = 128


def on_device(embeddings, centers, sample_ids, labels):
    section_count = lax.axis_size("section")
    batch_count = lax.axis_size("dp")
    class_count = lax.axis_size("cls")
    assert section_count == 2 and batch_count % 2 == 0
    section = lax.axis_index("section")
    batch = lax.axis_index("dp")
    cls = lax.axis_index("cls")
    shard_index = lax.axis_index(("section", "dp", "cls"))
    swap = [(0, 1), (1, 0)]
    per_shard = centers.shape[0]
    width = embeddings.shape[1]
    rows_per_batch = embeddings.shape[0]
    half = rows_per_batch // section_count
    devices = section_count * batch_count * class_count
    rows_here = rows_per_batch * batch_count // devices
    assert half == class_count * rows_here and rows_here >= 3 and half <= EXTRA and rows_here <= EXTRA

    my_rows = lax.dynamic_slice_in_dim(embeddings, section * half, half, 0)
    my_labels = lax.dynamic_slice_in_dim(labels, section * half, half, 0)
    pieces = jnp.stack([my_labels % 256, (my_labels // 256) % 256, my_labels // 65536], axis=1)
    packed = jnp.concatenate(
        [my_rows, pieces.astype(jnp.bfloat16), jnp.zeros((half, EXTRA - 3), jnp.bfloat16)], axis=1
    )
    packed = lax.all_to_all(
        jnp.broadcast_to(packed[None], (batch_count,) + packed.shape), "dp", 0, 0, tiled=False
    ).reshape(batch_count * half, width + EXTRA)
    gathered = packed[:, :width]
    received = packed[:, width : width + 3].astype(jnp.int32)
    label_all = received[:, 0] + 256 * received[:, 1] + 65536 * received[:, 2]

    local_ids = sample_ids[0]
    chosen = jnp.take(centers, local_ids, axis=0).astype(jnp.float32)
    center_norm = jnp.sqrt(jnp.sum(chosen * chosen, axis=1) + EPSILON)
    unit_centers = (chosen / center_norm[:, None]).astype(jnp.bfloat16)
    global_ids = local_ids + shard_index * per_shard
    partner_centers = lax.ppermute(unit_centers, "section", swap)
    partner_ids = lax.ppermute(global_ids, "section", swap)
    both_centers = jnp.concatenate([unit_centers, partner_centers], axis=0)
    both_ids = jnp.concatenate([global_ids, partner_ids], axis=0)

    emb_float = gathered.astype(jnp.float32)
    row_norm = jnp.sqrt(jnp.sum(emb_float * emb_float, axis=1) + EPSILON)
    unit_rows = (emb_float / row_norm[:, None]).astype(jnp.bfloat16)
    cosine = lax.dot_general(
        unit_rows, both_centers, (((1,), (1,)), ((), ())), preferred_element_type=jnp.float32
    )
    matches = both_ids[None, :] == label_all[:, None]
    logits = LOGIT_SCALE * cosine - LOGIT_SCALE * MARGIN * matches.astype(jnp.float32)
    exponent = jnp.exp(logits)
    total_part = jnp.sum(exponent, axis=1)
    target_part = jnp.sum(jnp.where(matches, logits, jnp.float32(0.0)), axis=1)
    weights = exponent.astype(jnp.bfloat16)
    unscaled = jnp.dot(weights, both_centers, preferred_element_type=jnp.float32)
    own_center = jnp.dot(matches.astype(jnp.bfloat16), both_centers, preferred_element_type=jnp.float32)

    h = batch_count // 2

    def to_dest(values):
        tail = values.shape[1:]
        values = values.reshape((2, h, class_count, rows_here) + tail)
        values = jnp.moveaxis(values, 2, 0)
        values = jnp.swapaxes(values, 1, 2)
        return values.reshape((class_count, batch_count, rows_here) + tail)

    def pad(values):
        return jnp.pad(values, [(0, 0)] * (values.ndim - 1) + [(0, EXTRA - values.shape[-1])])

    block_rows = jnp.broadcast_to(
        jnp.stack([pad(total_part.reshape(batch_count, half)), pad(target_part.reshape(batch_count, half))], axis=1)[None],
        (class_count, batch_count, 2, EXTRA),
    )
    own_totals = pad(to_dest(total_part))[:, :, None, :]
    extra = jnp.concatenate(
        [block_rows, own_totals, jnp.zeros((class_count, batch_count, rows_here - 3, EXTRA), jnp.float32)], axis=2
    )
    payload = jnp.concatenate([to_dest(unscaled), to_dest(own_center), extra], axis=3)
    payload = lax.all_to_all(payload, "cls", 0, 0, tiled=False).sum(0)
    summed = lax.all_to_all(payload, "dp", 0, 0, tiled=False).sum(0)

    half_total = summed[0, 2 * width : 2 * width + half]
    half_target = summed[1, 2 * width : 2 * width + half]
    other_total, other_target = lax.ppermute((half_total, half_target), "section", swap)
    first = section == 0
    block_total = jnp.where(first, jnp.concatenate([half_total, other_total]), jnp.concatenate([other_total, half_total]))
    block_target = jnp.where(first, jnp.concatenate([half_target, other_target]), jnp.concatenate([other_target, half_target]))
    row_loss = jnp.log(block_total) - block_target

    unscaled_rows = summed[:, :width]
    own_rows = summed[:, width : 2 * width]
    totals_here = summed[2, 2 * width : 2 * width + rows_here]
    unit_grad = LOGIT_SCALE * (unscaled_rows / totals_here[:, None] - own_rows)
    source_batch = (batch % 2) * h + batch // 2
    offset = source_batch * half + cls * rows_here
    emb_rows = lax.dynamic_slice_in_dim(emb_float, offset, rows_here, 0)
    norm_rows = lax.dynamic_slice_in_dim(row_norm, offset, rows_here, 0)
    unit_float = emb_rows / norm_rows[:, None]
    along = jnp.sum(unit_float * unit_grad, axis=1, keepdims=True)
    computed = (unit_grad - unit_float * along) / norm_rows[:, None]

    pairs = [
        (s * batch_count + e, (1 - s) * batch_count + (e ^ 1))
        for s in range(2)
        for e in range(batch_count)
        if e % 2 != s
    ]
    received = lax.ppermute(computed, ("section", "dp"), pairs)
    feature_grad = jnp.where(batch % 2 == section, computed, received)
    return (feature_grad, row_loss)


def solution(mesh):
    return jax.shard_map(
        on_device,
        mesh=mesh,
        in_specs=(
            P("dp", None),
            P(("section", "dp", "cls"), None),
            P(("section", "dp", "cls"), None),
            P("dp"),
        ),
        out_specs=(P(("section", "dp", "cls"), None), P("dp")),
        check_vma=False,
    )
```

```python
import jax
import jax.numpy as jnp
from jax import lax
from jax.sharding import PartitionSpec as P

LOGIT_SCALE = 64.0
MARGIN = 0.35
EPSILON = 1e-06
EXTRA = 128


def split_pair(values):
    high = values.astype(jnp.bfloat16)
    low = (values - high.astype(jnp.float32)).astype(jnp.bfloat16)
    return high, low


def reduce_stage(unscaled, own_center, extra, axis):
    width, more = unscaled.shape[-1], extra.shape[-1]
    unscaled_high, unscaled_low = split_pair(unscaled)
    extra_high, extra_low = split_pair(extra)
    packed = jnp.concatenate(
        [unscaled_high, unscaled_low, own_center.astype(jnp.bfloat16), extra_high, extra_low], axis=-1
    )
    packed = lax.all_to_all(packed, axis, 0, 0, tiled=False).astype(jnp.float32)
    unscaled = (packed[..., :width] + packed[..., width : 2 * width]).sum(0)
    own_center = packed[..., 2 * width : 3 * width].sum(0)
    extra = (packed[..., 3 * width : 3 * width + more] + packed[..., 3 * width + more :]).sum(0)
    return unscaled, own_center, extra


def on_device(embeddings, centers, sample_ids, labels):
    section_count = lax.axis_size("section")
    batch_count = lax.axis_size("dp")
    class_count = lax.axis_size("cls")
    assert section_count == 2 and batch_count % 2 == 0
    section = lax.axis_index("section")
    batch = lax.axis_index("dp")
    cls = lax.axis_index("cls")
    shard_index = lax.axis_index(("section", "dp", "cls"))
    swap = [(0, 1), (1, 0)]
    per_shard = centers.shape[0]
    width = embeddings.shape[1]
    rows_per_batch = embeddings.shape[0]
    half = rows_per_batch // section_count
    devices = section_count * batch_count * class_count
    rows_here = rows_per_batch * batch_count // devices
    assert half == class_count * rows_here and rows_here >= 3 and half <= EXTRA and rows_here <= EXTRA

    my_rows = lax.dynamic_slice_in_dim(embeddings, section * half, half, 0)
    my_labels = lax.dynamic_slice_in_dim(labels, section * half, half, 0)
    pieces = jnp.stack([my_labels % 256, (my_labels // 256) % 256, my_labels // 65536], axis=1)
    packed = jnp.concatenate(
        [my_rows, pieces.astype(jnp.bfloat16), jnp.zeros((half, EXTRA - 3), jnp.bfloat16)], axis=1
    )
    packed = lax.all_to_all(
        jnp.broadcast_to(packed[None], (batch_count,) + packed.shape), "dp", 0, 0, tiled=False
    ).reshape(batch_count * half, width + EXTRA)
    gathered = packed[:, :width]
    received = packed[:, width : width + 3].astype(jnp.int32)
    label_all = received[:, 0] + 256 * received[:, 1] + 65536 * received[:, 2]

    local_ids = sample_ids[0]
    chosen = jnp.take(centers, local_ids, axis=0).astype(jnp.float32)
    center_norm = jnp.sqrt(jnp.sum(chosen * chosen, axis=1) + EPSILON)
    unit_centers = (chosen / center_norm[:, None]).astype(jnp.bfloat16)
    global_ids = local_ids + shard_index * per_shard
    partner_centers = lax.ppermute(unit_centers, "section", swap)
    partner_ids = lax.ppermute(global_ids, "section", swap)
    both_centers = jnp.concatenate([unit_centers, partner_centers], axis=0)
    both_ids = jnp.concatenate([global_ids, partner_ids], axis=0)

    emb_float = gathered.astype(jnp.float32)
    row_norm = jnp.sqrt(jnp.sum(emb_float * emb_float, axis=1) + EPSILON)
    unit_rows = (emb_float / row_norm[:, None]).astype(jnp.bfloat16)
    cosine = lax.dot_general(
        unit_rows, both_centers, (((1,), (1,)), ((), ())), preferred_element_type=jnp.float32
    )
    matches = both_ids[None, :] == label_all[:, None]
    logits = LOGIT_SCALE * cosine - LOGIT_SCALE * MARGIN * matches.astype(jnp.float32)
    exponent = jnp.exp(logits)
    total_part = jnp.sum(exponent, axis=1)
    target_part = jnp.sum(jnp.where(matches, logits, jnp.float32(0.0)), axis=1)
    weights = exponent.astype(jnp.bfloat16)
    unscaled = jnp.dot(weights, both_centers, preferred_element_type=jnp.float32)
    own_center = jnp.dot(matches.astype(jnp.bfloat16), both_centers, preferred_element_type=jnp.float32)

    h = batch_count // 2

    def to_dest(values):
        tail = values.shape[1:]
        values = values.reshape((2, h, class_count, rows_here) + tail)
        values = jnp.moveaxis(values, 2, 0)
        values = jnp.swapaxes(values, 1, 2)
        return values.reshape((class_count, batch_count, rows_here) + tail)

    def pad(values):
        return jnp.pad(values, [(0, 0)] * (values.ndim - 1) + [(0, EXTRA - values.shape[-1])])

    block_rows = jnp.broadcast_to(
        jnp.stack([pad(total_part.reshape(batch_count, half)), pad(target_part.reshape(batch_count, half))], axis=1)[None],
        (class_count, batch_count, 2, EXTRA),
    )
    own_totals = pad(to_dest(total_part))[:, :, None, :]
    extra = jnp.concatenate(
        [block_rows, own_totals, jnp.zeros((class_count, batch_count, rows_here - 3, EXTRA), jnp.float32)], axis=2
    )
    unscaled, own_center, extra = to_dest(unscaled), to_dest(own_center), extra
    for axis in ("cls", "dp"):
        unscaled, own_center, extra = reduce_stage(unscaled, own_center, extra, axis)
    summed = jnp.concatenate([unscaled, own_center, extra], axis=-1)

    half_total = summed[0, 2 * width : 2 * width + half]
    half_target = summed[1, 2 * width : 2 * width + half]
    other_total, other_target = lax.ppermute((half_total, half_target), "section", swap)
    first = section == 0
    block_total = jnp.where(first, jnp.concatenate([half_total, other_total]), jnp.concatenate([other_total, half_total]))
    block_target = jnp.where(first, jnp.concatenate([half_target, other_target]), jnp.concatenate([other_target, half_target]))
    row_loss = jnp.log(block_total) - block_target

    unscaled_rows = summed[:, :width]
    own_rows = summed[:, width : 2 * width]
    totals_here = summed[2, 2 * width : 2 * width + rows_here]
    unit_grad = LOGIT_SCALE * (unscaled_rows / totals_here[:, None] - own_rows)
    source_batch = (batch % 2) * h + batch // 2
    offset = source_batch * half + cls * rows_here
    emb_rows = lax.dynamic_slice_in_dim(emb_float, offset, rows_here, 0)
    norm_rows = lax.dynamic_slice_in_dim(row_norm, offset, rows_here, 0)
    unit_float = emb_rows / norm_rows[:, None]
    along = jnp.sum(unit_float * unit_grad, axis=1, keepdims=True)
    computed = (unit_grad - unit_float * along) / norm_rows[:, None]

    pairs = [
        (s * batch_count + e, (1 - s) * batch_count + (e ^ 1))
        for s in range(2)
        for e in range(batch_count)
        if e % 2 != s
    ]
    received = lax.ppermute(computed, ("section", "dp"), pairs)
    feature_grad = jnp.where(batch % 2 == section, computed, received)
    return (feature_grad, row_loss)


def solution(mesh):
    return jax.shard_map(
        on_device,
        mesh=mesh,
        in_specs=(
            P("dp", None),
            P(("section", "dp", "cls"), None),
            P(("section", "dp", "cls"), None),
            P("dp"),
        ),
        out_specs=(P(("section", "dp", "cls"), None), P("dp")),
        check_vma=False,
    )
```

```python
import jax
import jax.numpy as jnp
from jax import lax
from jax.sharding import PartitionSpec as P

LOGIT_SCALE = 64.0
MARGIN = 0.35
EPSILON = 1e-06
EXTRA = 128


def split_pair(values):
    high = lax.reduce_precision(values, exponent_bits=8, mantissa_bits=7)
    low = (values - high).astype(jnp.bfloat16)
    return high.astype(jnp.bfloat16), low


def reduce_stage(unscaled, own_center, extra, axis):
    width, more = unscaled.shape[-1], extra.shape[-1]
    unscaled_high, unscaled_low = split_pair(unscaled)
    extra_high, extra_low = split_pair(extra)
    packed = jnp.concatenate(
        [unscaled_high, unscaled_low, own_center.astype(jnp.bfloat16), extra_high, extra_low], axis=-1
    )
    packed = lax.all_to_all(packed, axis, 0, 0, tiled=False).astype(jnp.float32)
    unscaled = (packed[..., :width] + packed[..., width : 2 * width]).sum(0)
    own_center = packed[..., 2 * width : 3 * width].sum(0)
    extra = (packed[..., 3 * width : 3 * width + more] + packed[..., 3 * width + more :]).sum(0)
    return unscaled, own_center, extra


def on_device(embeddings, centers, sample_ids, labels):
    section_count = lax.axis_size("section")
    batch_count = lax.axis_size("dp")
    class_count = lax.axis_size("cls")
    assert section_count == 2 and batch_count % 2 == 0
    section = lax.axis_index("section")
    batch = lax.axis_index("dp")
    cls = lax.axis_index("cls")
    shard_index = lax.axis_index(("section", "dp", "cls"))
    swap = [(0, 1), (1, 0)]
    per_shard = centers.shape[0]
    width = embeddings.shape[1]
    rows_per_batch = embeddings.shape[0]
    half = rows_per_batch // section_count
    devices = section_count * batch_count * class_count
    rows_here = rows_per_batch * batch_count // devices
    assert half == class_count * rows_here and rows_here >= 3 and half <= EXTRA and rows_here <= EXTRA

    my_rows = lax.dynamic_slice_in_dim(embeddings, section * half, half, 0)
    my_labels = lax.dynamic_slice_in_dim(labels, section * half, half, 0)
    pieces = jnp.stack([my_labels % 256, (my_labels // 256) % 256, my_labels // 65536], axis=1)
    packed = jnp.concatenate(
        [my_rows, pieces.astype(jnp.bfloat16), jnp.zeros((half, EXTRA - 3), jnp.bfloat16)], axis=1
    )
    packed = lax.all_to_all(
        jnp.broadcast_to(packed[None], (batch_count,) + packed.shape), "dp", 0, 0, tiled=False
    ).reshape(batch_count * half, width + EXTRA)
    gathered = packed[:, :width]
    received = packed[:, width : width + 3].astype(jnp.int32)
    label_all = received[:, 0] + 256 * received[:, 1] + 65536 * received[:, 2]

    local_ids = sample_ids[0]
    chosen = jnp.take(centers, local_ids, axis=0).astype(jnp.float32)
    center_norm = jnp.sqrt(jnp.sum(chosen * chosen, axis=1) + EPSILON)
    unit_centers = (chosen / center_norm[:, None]).astype(jnp.bfloat16)
    global_ids = local_ids + shard_index * per_shard
    partner_centers = lax.ppermute(unit_centers, "section", swap)
    partner_ids = lax.ppermute(global_ids, "section", swap)
    both_centers = jnp.concatenate([unit_centers, partner_centers], axis=0)
    both_ids = jnp.concatenate([global_ids, partner_ids], axis=0)

    emb_float = gathered.astype(jnp.float32)
    row_norm = jnp.sqrt(jnp.sum(emb_float * emb_float, axis=1) + EPSILON)
    unit_rows = (emb_float / row_norm[:, None]).astype(jnp.bfloat16)
    cosine = lax.dot_general(
        unit_rows, both_centers, (((1,), (1,)), ((), ())), preferred_element_type=jnp.float32
    )
    matches = both_ids[None, :] == label_all[:, None]
    logits = LOGIT_SCALE * cosine - LOGIT_SCALE * MARGIN * matches.astype(jnp.float32)
    exponent = jnp.exp(logits)
    total_part = jnp.sum(exponent, axis=1)
    target_part = jnp.sum(jnp.where(matches, logits, jnp.float32(0.0)), axis=1)
    weights = exponent.astype(jnp.bfloat16)
    unscaled = jnp.dot(weights, both_centers, preferred_element_type=jnp.float32)
    own_center = jnp.dot(matches.astype(jnp.bfloat16), both_centers, preferred_element_type=jnp.float32)

    h = batch_count // 2

    def to_dest(values):
        tail = values.shape[1:]
        values = values.reshape((2, h, class_count, rows_here) + tail)
        values = jnp.moveaxis(values, 2, 0)
        values = jnp.swapaxes(values, 1, 2)
        return values.reshape((class_count, batch_count, rows_here) + tail)

    def pad(values):
        return jnp.pad(values, [(0, 0)] * (values.ndim - 1) + [(0, EXTRA - values.shape[-1])])

    block_rows = jnp.broadcast_to(
        jnp.stack([pad(total_part.reshape(batch_count, half)), pad(target_part.reshape(batch_count, half))], axis=1)[None],
        (class_count, batch_count, 2, EXTRA),
    )
    own_totals = pad(to_dest(total_part))[:, :, None, :]
    extra = jnp.concatenate(
        [block_rows, own_totals, jnp.zeros((class_count, batch_count, rows_here - 3, EXTRA), jnp.float32)], axis=2
    )
    unscaled, own_center, extra = to_dest(unscaled), to_dest(own_center), extra
    for axis in ("cls", "dp"):
        unscaled, own_center, extra = reduce_stage(unscaled, own_center, extra, axis)
    summed = jnp.concatenate([unscaled, own_center, extra], axis=-1)

    half_total = summed[0, 2 * width : 2 * width + half]
    half_target = summed[1, 2 * width : 2 * width + half]
    other_total, other_target = lax.ppermute((half_total, half_target), "section", swap)
    first = section == 0
    block_total = jnp.where(first, jnp.concatenate([half_total, other_total]), jnp.concatenate([other_total, half_total]))
    block_target = jnp.where(first, jnp.concatenate([half_target, other_target]), jnp.concatenate([other_target, half_target]))
    row_loss = jnp.log(block_total) - block_target

    unscaled_rows = summed[:, :width]
    own_rows = summed[:, width : 2 * width]
    totals_here = summed[2, 2 * width : 2 * width + rows_here]
    unit_grad = LOGIT_SCALE * (unscaled_rows / totals_here[:, None] - own_rows)
    source_batch = (batch % 2) * h + batch // 2
    offset = source_batch * half + cls * rows_here
    emb_rows = lax.dynamic_slice_in_dim(emb_float, offset, rows_here, 0)
    norm_rows = lax.dynamic_slice_in_dim(row_norm, offset, rows_here, 0)
    unit_float = emb_rows / norm_rows[:, None]
    along = jnp.sum(unit_float * unit_grad, axis=1, keepdims=True)
    computed = (unit_grad - unit_float * along) / norm_rows[:, None]

    pairs = [
        (s * batch_count + e, (1 - s) * batch_count + (e ^ 1))
        for s in range(2)
        for e in range(batch_count)
        if e % 2 != s
    ]
    received = lax.ppermute(computed, ("section", "dp"), pairs)
    feature_grad = jnp.where(batch % 2 == section, computed, received)
    return (feature_grad, row_loss)


def solution(mesh):
    return jax.shard_map(
        on_device,
        mesh=mesh,
        in_specs=(
            P("dp", None),
            P(("section", "dp", "cls"), None),
            P(("section", "dp", "cls"), None),
            P("dp"),
        ),
        out_specs=(P(("section", "dp", "cls"), None), P("dp")),
        check_vma=False,
    )
```

```python
import jax
import jax.numpy as jnp
from jax import lax
from jax.sharding import PartitionSpec as P

LOGIT_SCALE = 64.0
MARGIN = 0.35
EPSILON = 1e-06
EXTRA = 128
CHUNKS = 2


def split_pair(values):
    high = lax.reduce_precision(values, exponent_bits=8, mantissa_bits=7)
    low = (values - high).astype(jnp.bfloat16)
    return high.astype(jnp.bfloat16), low


def reduce_stage(unscaled, own_center, extra, axis):
    width, more = unscaled.shape[-1], extra.shape[-1]
    unscaled_high, unscaled_low = split_pair(unscaled)
    extra_high, extra_low = split_pair(extra)
    packed = jnp.concatenate(
        [unscaled_high, unscaled_low, own_center.astype(jnp.bfloat16), extra_high, extra_low], axis=-1
    )
    packed = lax.all_to_all(packed, axis, 0, 0, tiled=False).astype(jnp.float32)
    unscaled = (packed[..., :width] + packed[..., width : 2 * width]).sum(0)
    own_center = packed[..., 2 * width : 3 * width].sum(0)
    extra = (packed[..., 3 * width : 3 * width + more] + packed[..., 3 * width + more :]).sum(0)
    return unscaled, own_center, extra


def on_device(embeddings, centers, sample_ids, labels):
    section_count = lax.axis_size("section")
    batch_count = lax.axis_size("dp")
    class_count = lax.axis_size("cls")
    assert section_count == 2 and batch_count % 2 == 0
    section = lax.axis_index("section")
    batch = lax.axis_index("dp")
    cls = lax.axis_index("cls")
    shard_index = lax.axis_index(("section", "dp", "cls"))
    swap = [(0, 1), (1, 0)]
    per_shard = centers.shape[0]
    width = embeddings.shape[1]
    rows_per_batch = embeddings.shape[0]
    half = rows_per_batch // section_count
    devices = section_count * batch_count * class_count
    rows_here = rows_per_batch * batch_count // devices
    piece = rows_here // CHUNKS
    assert half == class_count * rows_here and rows_here % CHUNKS == 0 and piece >= 3
    assert half <= EXTRA and rows_here <= EXTRA

    my_rows = lax.dynamic_slice_in_dim(embeddings, section * half, half, 0)
    my_labels = lax.dynamic_slice_in_dim(labels, section * half, half, 0)
    pieces = jnp.stack([my_labels % 256, (my_labels // 256) % 256, my_labels // 65536], axis=1)
    packed = jnp.concatenate(
        [my_rows, pieces.astype(jnp.bfloat16), jnp.zeros((half, EXTRA - 3), jnp.bfloat16)], axis=1
    )
    packed = lax.all_to_all(
        jnp.broadcast_to(packed[None], (batch_count,) + packed.shape), "dp", 0, 0, tiled=False
    ).reshape(batch_count * half, width + EXTRA)
    gathered = packed[:, :width]
    received = packed[:, width : width + 3].astype(jnp.int32)
    label_all = received[:, 0] + 256 * received[:, 1] + 65536 * received[:, 2]

    local_ids = sample_ids[0]
    chosen = jnp.take(centers, local_ids, axis=0).astype(jnp.float32)
    center_norm = jnp.sqrt(jnp.sum(chosen * chosen, axis=1) + EPSILON)
    unit_centers = (chosen / center_norm[:, None]).astype(jnp.bfloat16)
    global_ids = local_ids + shard_index * per_shard
    partner_centers = lax.ppermute(unit_centers, "section", swap)
    partner_ids = lax.ppermute(global_ids, "section", swap)
    both_centers = jnp.concatenate([unit_centers, partner_centers], axis=0)
    both_ids = jnp.concatenate([global_ids, partner_ids], axis=0)

    emb_float = gathered.astype(jnp.float32)
    row_norm = jnp.sqrt(jnp.sum(emb_float * emb_float, axis=1) + EPSILON)
    unit_rows = (emb_float / row_norm[:, None]).astype(jnp.bfloat16)
    h = batch_count // 2

    def pad(values):
        return jnp.pad(values, [(0, 0)] * (values.ndim - 1) + [(0, EXTRA - values.shape[-1])])

    def to_dest(values):
        tail = values.shape[3:]
        values = values.reshape((2, h, class_count, piece) + tail)
        values = jnp.moveaxis(values, 2, 0)
        values = jnp.swapaxes(values, 1, 2)
        return values.reshape((class_count, batch_count, piece) + tail)

    row_view = unit_rows.reshape(batch_count, class_count, rows_here, width)
    label_view = label_all.reshape(batch_count, class_count, rows_here)
    results = []
    for k in range(CHUNKS):
        chunk_rows = row_view[:, :, k * piece : (k + 1) * piece].reshape(-1, width)
        chunk_labels = label_view[:, :, k * piece : (k + 1) * piece].reshape(-1)
        cosine = lax.dot_general(
            chunk_rows, both_centers, (((1,), (1,)), ((), ())), preferred_element_type=jnp.float32
        )
        matches = both_ids[None, :] == chunk_labels[:, None]
        logits = LOGIT_SCALE * cosine - LOGIT_SCALE * MARGIN * matches.astype(jnp.float32)
        exponent = jnp.exp(logits)
        total_part = jnp.sum(exponent, axis=1)
        target_part = jnp.sum(jnp.where(matches, logits, jnp.float32(0.0)), axis=1)
        weights = exponent.astype(jnp.bfloat16)
        unscaled = jnp.dot(weights, both_centers, preferred_element_type=jnp.float32)
        own_center = jnp.dot(matches.astype(jnp.bfloat16), both_centers, preferred_element_type=jnp.float32)
        shape4 = (batch_count, class_count, piece)
        block_rows = jnp.broadcast_to(
            jnp.stack(
                [pad(total_part.reshape(batch_count, -1)), pad(target_part.reshape(batch_count, -1))], axis=1
            )[None],
            (class_count, batch_count, 2, EXTRA),
        )
        own_totals = pad(to_dest(total_part.reshape(shape4)))[:, :, None, :]
        extra = jnp.concatenate(
            [block_rows, own_totals, jnp.zeros((class_count, batch_count, piece - 3, EXTRA), jnp.float32)], axis=2
        )
        parts = (to_dest(unscaled.reshape(shape4 + (width,))), to_dest(own_center.reshape(shape4 + (width,))), extra)
        for axis in ("cls", "dp"):
            parts = reduce_stage(*parts, axis)
        results.append(parts)

    def block_values(row):
        per_chunk = [r[2][row, : class_count * piece].reshape(class_count, piece) for r in results]
        return jnp.concatenate(per_chunk, axis=1).reshape(-1)

    half_total = block_values(0)
    half_target = block_values(1)
    other_total, other_target = lax.ppermute((half_total, half_target), "section", swap)
    first = section == 0
    block_total = jnp.where(first, jnp.concatenate([half_total, other_total]), jnp.concatenate([other_total, half_total]))
    block_target = jnp.where(first, jnp.concatenate([half_target, other_target]), jnp.concatenate([other_target, half_target]))
    row_loss = jnp.log(block_total) - block_target

    unscaled_rows = jnp.concatenate([r[0] for r in results], axis=0)
    own_rows = jnp.concatenate([r[1] for r in results], axis=0)
    totals_here = jnp.concatenate([r[2][2, :piece] for r in results], axis=0)
    unit_grad = LOGIT_SCALE * (unscaled_rows / totals_here[:, None] - own_rows)
    source_batch = (batch % 2) * h + batch // 2
    offset = source_batch * half + cls * rows_here
    emb_rows = lax.dynamic_slice_in_dim(emb_float, offset, rows_here, 0)
    norm_rows = lax.dynamic_slice_in_dim(row_norm, offset, rows_here, 0)
    unit_float = emb_rows / norm_rows[:, None]
    along = jnp.sum(unit_float * unit_grad, axis=1, keepdims=True)
    computed = (unit_grad - unit_float * along) / norm_rows[:, None]

    pairs = [
        (s * batch_count + e, (1 - s) * batch_count + (e ^ 1))
        for s in range(2)
        for e in range(batch_count)
        if e % 2 != s
    ]
    received_grad = lax.ppermute(computed, ("section", "dp"), pairs)
    feature_grad = jnp.where(batch % 2 == section, computed, received_grad)
    return (feature_grad, row_loss)


def solution(mesh):
    return jax.shard_map(
        on_device,
        mesh=mesh,
        in_specs=(
            P("dp", None),
            P(("section", "dp", "cls"), None),
            P(("section", "dp", "cls"), None),
            P("dp"),
        ),
        out_specs=(P(("section", "dp", "cls"), None), P("dp")),
        check_vma=False,
    )
```

```python
import jax
import jax.numpy as jnp
from jax import lax
from jax.sharding import PartitionSpec as P

LOGIT_SCALE = 64.0
MARGIN = 0.35
EPSILON = 1e-06
EXTRA = 128


def split_pair(values):
    high = lax.reduce_precision(values, exponent_bits=8, mantissa_bits=7)
    low = (values - high).astype(jnp.bfloat16)
    return high.astype(jnp.bfloat16), low


def reduce_stage(unscaled, own_center, extra, axis):
    width, rows = unscaled.shape[-1], extra.shape[-2]
    unscaled_high, unscaled_low = split_pair(unscaled)
    extra_high, extra_low = split_pair(extra[..., :3, :])
    spare = jnp.zeros(extra.shape[:-2] + (rows - 6, extra.shape[-1]), jnp.bfloat16)
    extra_packed = jnp.concatenate([extra_high, extra_low, spare], axis=-2)
    packed = jnp.concatenate(
        [unscaled_high, unscaled_low, own_center.astype(jnp.bfloat16), extra_packed], axis=-1
    )
    packed = lax.all_to_all(packed, axis, 0, 0, tiled=False).astype(jnp.float32)
    unscaled = (packed[..., :width] + packed[..., width : 2 * width]).sum(0)
    own_center = packed[..., 2 * width : 3 * width].sum(0)
    extra_sum = (packed[..., 3 * width :][..., :3, :] + packed[..., 3 * width :][..., 3:6, :]).sum(0)
    extra = jnp.concatenate([extra_sum, jnp.zeros(extra_sum.shape[:-2] + (rows - 3, extra_sum.shape[-1]), jnp.float32)], axis=-2)
    return unscaled, own_center, extra


def on_device(embeddings, centers, sample_ids, labels):
    section_count = lax.axis_size("section")
    batch_count = lax.axis_size("dp")
    class_count = lax.axis_size("cls")
    assert section_count == 2 and batch_count % 2 == 0
    section = lax.axis_index("section")
    batch = lax.axis_index("dp")
    cls = lax.axis_index("cls")
    shard_index = lax.axis_index(("section", "dp", "cls"))
    swap = [(0, 1), (1, 0)]
    per_shard = centers.shape[0]
    width = embeddings.shape[1]
    rows_per_batch = embeddings.shape[0]
    half = rows_per_batch // section_count
    devices = section_count * batch_count * class_count
    rows_here = rows_per_batch * batch_count // devices
    assert half == class_count * rows_here and rows_here >= 6 and half <= EXTRA and rows_here <= EXTRA

    my_rows = lax.dynamic_slice_in_dim(embeddings, section * half, half, 0)
    my_labels = lax.dynamic_slice_in_dim(labels, section * half, half, 0)
    pieces = jnp.stack([my_labels % 256, (my_labels // 256) % 256, my_labels // 65536], axis=1)
    packed = jnp.concatenate(
        [my_rows, pieces.astype(jnp.bfloat16), jnp.zeros((half, EXTRA - 3), jnp.bfloat16)], axis=1
    )
    packed = lax.all_to_all(
        jnp.broadcast_to(packed[None], (batch_count,) + packed.shape), "dp", 0, 0, tiled=False
    ).reshape(batch_count * half, width + EXTRA)
    gathered = packed[:, :width]
    received = packed[:, width : width + 3].astype(jnp.int32)
    label_all = received[:, 0] + 256 * received[:, 1] + 65536 * received[:, 2]

    local_ids = sample_ids[0]
    chosen = jnp.take(centers, local_ids, axis=0).astype(jnp.float32)
    center_norm = jnp.sqrt(jnp.sum(chosen * chosen, axis=1) + EPSILON)
    unit_centers = (chosen / center_norm[:, None]).astype(jnp.bfloat16)
    global_ids = local_ids + shard_index * per_shard
    partner_centers = lax.ppermute(unit_centers, "section", swap)
    partner_ids = lax.ppermute(global_ids, "section", swap)
    both_centers = jnp.concatenate([unit_centers, partner_centers], axis=0)
    both_ids = jnp.concatenate([global_ids, partner_ids], axis=0)

    emb_float = gathered.astype(jnp.float32)
    row_norm = jnp.sqrt(jnp.sum(emb_float * emb_float, axis=1) + EPSILON)
    unit_rows = (emb_float / row_norm[:, None]).astype(jnp.bfloat16)
    cosine = lax.dot_general(
        unit_rows, both_centers, (((1,), (1,)), ((), ())), preferred_element_type=jnp.float32
    )
    matches = both_ids[None, :] == label_all[:, None]
    logits = LOGIT_SCALE * cosine - LOGIT_SCALE * MARGIN * matches.astype(jnp.float32)
    exponent = jnp.exp(logits)
    total_part = jnp.sum(exponent, axis=1)
    target_part = jnp.sum(jnp.where(matches, logits, jnp.float32(0.0)), axis=1)
    weights = exponent.astype(jnp.bfloat16)
    unscaled = jnp.dot(weights, both_centers, preferred_element_type=jnp.float32)
    own_center = jnp.dot(matches.astype(jnp.bfloat16), both_centers, preferred_element_type=jnp.float32)

    h = batch_count // 2

    def to_dest(values):
        tail = values.shape[1:]
        values = values.reshape((2, h, class_count, rows_here) + tail)
        values = jnp.moveaxis(values, 2, 0)
        values = jnp.swapaxes(values, 1, 2)
        return values.reshape((class_count, batch_count, rows_here) + tail)

    def pad(values):
        return jnp.pad(values, [(0, 0)] * (values.ndim - 1) + [(0, EXTRA - values.shape[-1])])

    block_rows = jnp.broadcast_to(
        jnp.stack([pad(total_part.reshape(batch_count, half)), pad(target_part.reshape(batch_count, half))], axis=1)[None],
        (class_count, batch_count, 2, EXTRA),
    )
    own_totals = pad(to_dest(total_part))[:, :, None, :]
    extra = jnp.concatenate(
        [block_rows, own_totals, jnp.zeros((class_count, batch_count, rows_here - 3, EXTRA), jnp.float32)], axis=2
    )
    unscaled, own_center, extra = to_dest(unscaled), to_dest(own_center), extra
    for axis in ("cls", "dp"):
        unscaled, own_center, extra = reduce_stage(unscaled, own_center, extra, axis)
    summed = jnp.concatenate([unscaled, own_center, extra], axis=-1)

    half_total = summed[0, 2 * width : 2 * width + half]
    half_target = summed[1, 2 * width : 2 * width + half]
    other_total, other_target = lax.ppermute((half_total, half_target), "section", swap)
    first = section == 0
    block_total = jnp.where(first, jnp.concatenate([half_total, other_total]), jnp.concatenate([other_total, half_total]))
    block_target = jnp.where(first, jnp.concatenate([half_target, other_target]), jnp.concatenate([other_target, half_target]))
    row_loss = jnp.log(block_total) - block_target

    unscaled_rows = summed[:, :width]
    own_rows = summed[:, width : 2 * width]
    totals_here = summed[2, 2 * width : 2 * width + rows_here]
    unit_grad = LOGIT_SCALE * (unscaled_rows / totals_here[:, None] - own_rows)
    source_batch = (batch % 2) * h + batch // 2
    offset = source_batch * half + cls * rows_here
    emb_rows = lax.dynamic_slice_in_dim(emb_float, offset, rows_here, 0)
    norm_rows = lax.dynamic_slice_in_dim(row_norm, offset, rows_here, 0)
    unit_float = emb_rows / norm_rows[:, None]
    along = jnp.sum(unit_float * unit_grad, axis=1, keepdims=True)
    computed = (unit_grad - unit_float * along) / norm_rows[:, None]

    pairs = [
        (s * batch_count + e, (1 - s) * batch_count + (e ^ 1))
        for s in range(2)
        for e in range(batch_count)
        if e % 2 != s
    ]
    received = lax.ppermute(computed, ("section", "dp"), pairs)
    feature_grad = jnp.where(batch % 2 == section, computed, received)
    return (feature_grad, row_loss)


def solution(mesh):
    return jax.shard_map(
        on_device,
        mesh=mesh,
        in_specs=(
            P("dp", None),
            P(("section", "dp", "cls"), None),
            P(("section", "dp", "cls"), None),
            P("dp"),
        ),
        out_specs=(P(("section", "dp", "cls"), None), P("dp")),
        check_vma=False,
    )
```

```python
import jax
import jax.numpy as jnp
from jax import lax
from jax.sharding import PartitionSpec as P

LOGIT_SCALE = 64.0
MARGIN = 0.35
EPSILON = 1e-06
EXTRA = 128


def split_pair(values):
    high = lax.reduce_precision(values, exponent_bits=8, mantissa_bits=7)
    low = (values - high).astype(jnp.bfloat16)
    return high.astype(jnp.bfloat16), low


def reduce_stage(unscaled, own_center, extra, axis):
    width, rows = unscaled.shape[-1], extra.shape[-2]
    unscaled_high, unscaled_low = split_pair(unscaled)
    extra_high, extra_low = split_pair(extra[..., :3, :])
    spare = jnp.zeros(extra.shape[:-2] + (rows - 6, extra.shape[-1]), jnp.bfloat16)
    extra_packed = jnp.concatenate([extra_high, extra_low, spare], axis=-2)
    packed = jnp.concatenate(
        [unscaled_high, unscaled_low, own_center.astype(jnp.bfloat16), extra_packed], axis=-1
    )
    packed = lax.all_to_all(packed, axis, 0, 0, tiled=False).astype(jnp.float32)
    unscaled = (packed[..., :width] + packed[..., width : 2 * width]).sum(0)
    own_center = packed[..., 2 * width : 3 * width].sum(0)
    extra_sum = (packed[..., 3 * width :][..., :3, :] + packed[..., 3 * width :][..., 3:6, :]).sum(0)
    extra = jnp.concatenate([extra_sum, jnp.zeros(extra_sum.shape[:-2] + (rows - 3, extra_sum.shape[-1]), jnp.float32)], axis=-2)
    return unscaled, own_center, extra


def on_device(embeddings, centers, sample_ids, labels):
    section_count = lax.axis_size("section")
    batch_count = lax.axis_size("dp")
    class_count = lax.axis_size("cls")
    assert section_count == 2 and batch_count % 2 == 0
    section = lax.axis_index("section")
    batch = lax.axis_index("dp")
    cls = lax.axis_index("cls")
    shard_index = lax.axis_index(("section", "dp", "cls"))
    swap = [(0, 1), (1, 0)]
    per_shard = centers.shape[0]
    width = embeddings.shape[1]
    rows_per_batch = embeddings.shape[0]
    half = rows_per_batch // section_count
    devices = section_count * batch_count * class_count
    rows_here = rows_per_batch * batch_count // devices
    assert half == class_count * rows_here and rows_here >= 6 and half <= EXTRA and rows_here <= EXTRA

    my_rows = lax.dynamic_slice_in_dim(embeddings, section * half, half, 0)
    my_labels = lax.dynamic_slice_in_dim(labels, section * half, half, 0)
    pieces = jnp.stack([my_labels % 256, (my_labels // 256) % 256, my_labels // 65536], axis=1)
    packed = jnp.concatenate(
        [my_rows, pieces.astype(jnp.bfloat16), jnp.zeros((half, EXTRA - 3), jnp.bfloat16)], axis=1
    )
    packed = lax.all_to_all(
        jnp.broadcast_to(packed[None], (batch_count,) + packed.shape), "dp", 0, 0, tiled=False
    ).reshape(batch_count * half, width + EXTRA)
    gathered = packed[:, :width]
    received = packed[:, width : width + 3].astype(jnp.int32)
    label_all = received[:, 0] + 256 * received[:, 1] + 65536 * received[:, 2]

    local_ids = sample_ids[0]
    chosen = jnp.take(centers, local_ids, axis=0).astype(jnp.float32)
    center_norm = jnp.sqrt(jnp.sum(chosen * chosen, axis=1) + EPSILON)
    unit_centers = (chosen / center_norm[:, None]).astype(jnp.bfloat16)
    global_ids = local_ids + shard_index * per_shard
    partner_centers = lax.ppermute(unit_centers, "section", swap)
    partner_ids = lax.ppermute(global_ids, "section", swap)
    both_centers = jnp.concatenate([unit_centers, partner_centers], axis=0)
    both_ids = jnp.concatenate([global_ids, partner_ids], axis=0)

    emb_float = gathered.astype(jnp.float32)
    row_norm = jnp.sqrt(jnp.sum(emb_float * emb_float, axis=1) + EPSILON)
    unit_rows = (emb_float / row_norm[:, None]).astype(jnp.bfloat16)
    cosine = lax.dot_general(
        unit_rows, both_centers, (((1,), (1,)), ((), ())), preferred_element_type=jnp.float32
    )
    matches = both_ids[None, :] == label_all[:, None]
    logits = LOGIT_SCALE * cosine - LOGIT_SCALE * MARGIN * matches.astype(jnp.float32)
    exponent = jnp.exp(logits)
    total_part = jnp.sum(exponent, axis=1)
    target_part = jnp.sum(jnp.where(matches, logits, jnp.float32(0.0)), axis=1)
    weights = exponent.astype(jnp.bfloat16)
    stacked = jnp.concatenate([weights, matches.astype(jnp.bfloat16)], axis=0)
    products = jnp.dot(stacked, both_centers, preferred_element_type=jnp.float32)
    unscaled, own_center = products[: weights.shape[0]], products[weights.shape[0] :]

    h = batch_count // 2

    def to_dest(values):
        tail = values.shape[1:]
        values = values.reshape((2, h, class_count, rows_here) + tail)
        values = jnp.moveaxis(values, 2, 0)
        values = jnp.swapaxes(values, 1, 2)
        return values.reshape((class_count, batch_count, rows_here) + tail)

    def pad(values):
        return jnp.pad(values, [(0, 0)] * (values.ndim - 1) + [(0, EXTRA - values.shape[-1])])

    block_rows = jnp.broadcast_to(
        jnp.stack([pad(total_part.reshape(batch_count, half)), pad(target_part.reshape(batch_count, half))], axis=1)[None],
        (class_count, batch_count, 2, EXTRA),
    )
    own_totals = pad(to_dest(total_part))[:, :, None, :]
    extra = jnp.concatenate(
        [block_rows, own_totals, jnp.zeros((class_count, batch_count, rows_here - 3, EXTRA), jnp.float32)], axis=2
    )
    unscaled, own_center, extra = to_dest(unscaled), to_dest(own_center), extra
    for axis in ("cls", "dp"):
        unscaled, own_center, extra = reduce_stage(unscaled, own_center, extra, axis)
    summed = jnp.concatenate([unscaled, own_center, extra], axis=-1)

    half_total = summed[0, 2 * width : 2 * width + half]
    half_target = summed[1, 2 * width : 2 * width + half]
    other_total, other_target = lax.ppermute((half_total, half_target), "section", swap)
    first = section == 0
    block_total = jnp.where(first, jnp.concatenate([half_total, other_total]), jnp.concatenate([other_total, half_total]))
    block_target = jnp.where(first, jnp.concatenate([half_target, other_target]), jnp.concatenate([other_target, half_target]))
    row_loss = jnp.log(block_total) - block_target

    unscaled_rows = summed[:, :width]
    own_rows = summed[:, width : 2 * width]
    totals_here = summed[2, 2 * width : 2 * width + rows_here]
    unit_grad = LOGIT_SCALE * (unscaled_rows / totals_here[:, None] - own_rows)
    source_batch = (batch % 2) * h + batch // 2
    offset = source_batch * half + cls * rows_here
    emb_rows = lax.dynamic_slice_in_dim(emb_float, offset, rows_here, 0)
    norm_rows = lax.dynamic_slice_in_dim(row_norm, offset, rows_here, 0)
    unit_float = emb_rows / norm_rows[:, None]
    along = jnp.sum(unit_float * unit_grad, axis=1, keepdims=True)
    computed = (unit_grad - unit_float * along) / norm_rows[:, None]

    pairs = [
        (s * batch_count + e, (1 - s) * batch_count + (e ^ 1))
        for s in range(2)
        for e in range(batch_count)
        if e % 2 != s
    ]
    received = lax.ppermute(computed, ("section", "dp"), pairs)
    feature_grad = jnp.where(batch % 2 == section, computed, received)
    return (feature_grad, row_loss)


def solution(mesh):
    return jax.shard_map(
        on_device,
        mesh=mesh,
        in_specs=(
            P("dp", None),
            P(("section", "dp", "cls"), None),
            P(("section", "dp", "cls"), None),
            P("dp"),
        ),
        out_specs=(P(("section", "dp", "cls"), None), P("dp")),
        check_vma=False,
    )
```

```python
import jax
import jax.numpy as jnp
from jax import lax
from jax.sharding import PartitionSpec as P

LOGIT_SCALE = 64.0
MARGIN = 0.35
EPSILON = 1e-06
EXTRA = 128


def split_pair(values):
    high = lax.reduce_precision(values, exponent_bits=8, mantissa_bits=7)
    low = (values - high).astype(jnp.bfloat16)
    return high.astype(jnp.bfloat16), low


def reduce_stage(unscaled, own_center, extra, axis):
    width, rows = unscaled.shape[-1], extra.shape[-2]
    unscaled_high, unscaled_low = split_pair(unscaled)
    extra_high, extra_low = split_pair(extra[..., :3, :])
    spare = jnp.zeros(extra.shape[:-2] + (rows - 6, extra.shape[-1]), jnp.bfloat16)
    extra_packed = jnp.concatenate([extra_high, extra_low, spare], axis=-2)
    packed = jnp.concatenate(
        [unscaled_high, unscaled_low, own_center.astype(jnp.bfloat16), extra_packed], axis=-1
    )
    packed = lax.all_to_all(packed, axis, 0, 0, tiled=False).astype(jnp.float32)
    unscaled = (packed[..., :width] + packed[..., width : 2 * width]).sum(0)
    own_center = packed[..., 2 * width : 3 * width].sum(0)
    extra_sum = (packed[..., 3 * width :][..., :3, :] + packed[..., 3 * width :][..., 3:6, :]).sum(0)
    extra = jnp.concatenate([extra_sum, jnp.zeros(extra_sum.shape[:-2] + (rows - 3, extra_sum.shape[-1]), jnp.float32)], axis=-2)
    return unscaled, own_center, extra


def on_device(embeddings, centers, sample_ids, labels):
    section_count = lax.axis_size("section")
    batch_count = lax.axis_size("dp")
    class_count = lax.axis_size("cls")
    assert section_count == 2 and batch_count % 2 == 0
    section = lax.axis_index("section")
    batch = lax.axis_index("dp")
    cls = lax.axis_index("cls")
    shard_index = lax.axis_index(("section", "dp", "cls"))
    swap = [(0, 1), (1, 0)]
    per_shard = centers.shape[0]
    width = embeddings.shape[1]
    rows_per_batch = embeddings.shape[0]
    half = rows_per_batch // section_count
    devices = section_count * batch_count * class_count
    rows_here = rows_per_batch * batch_count // devices
    assert half == class_count * rows_here and rows_here >= 6 and half <= EXTRA and rows_here <= EXTRA

    my_rows = lax.dynamic_slice_in_dim(embeddings, section * half, half, 0)
    my_labels = lax.dynamic_slice_in_dim(labels, section * half, half, 0)
    pieces = jnp.stack([my_labels % 256, (my_labels // 256) % 256, my_labels // 65536], axis=1)
    packed = jnp.concatenate(
        [my_rows, pieces.astype(jnp.bfloat16), jnp.zeros((half, EXTRA - 3), jnp.bfloat16)], axis=1
    )
    packed = lax.all_to_all(
        jnp.broadcast_to(packed[None], (batch_count,) + packed.shape), "dp", 0, 0, tiled=False
    ).reshape(batch_count * half, width + EXTRA)
    gathered = packed[:, :width]
    received = packed[:, width : width + 3].astype(jnp.int32)
    label_all = received[:, 0] + 256 * received[:, 1] + 65536 * received[:, 2]

    local_ids = sample_ids[0]
    chosen = jnp.take(centers, local_ids, axis=0).astype(jnp.float32)
    center_norm = jnp.sqrt(jnp.sum(chosen * chosen, axis=1) + EPSILON)
    unit_centers = (chosen / center_norm[:, None]).astype(jnp.bfloat16)
    global_ids = local_ids + shard_index * per_shard
    partner_centers = lax.ppermute(unit_centers, "section", swap)
    partner_ids = lax.ppermute(global_ids, "section", swap)
    both_centers = jnp.concatenate([unit_centers, partner_centers], axis=0)
    both_ids = jnp.concatenate([global_ids, partner_ids], axis=0)

    emb_float = gathered.astype(jnp.float32)
    row_norm = jnp.sqrt(jnp.sum(emb_float * emb_float, axis=1) + EPSILON)
    unit_rows = (emb_float / row_norm[:, None]).astype(jnp.bfloat16)
    cosine = lax.dot_general(
        unit_rows, both_centers, (((1,), (1,)), ((), ())), preferred_element_type=jnp.float32
    )
    matches = both_ids[None, :] == label_all[:, None]
    logits = LOGIT_SCALE * cosine - LOGIT_SCALE * MARGIN * matches.astype(jnp.float32)
    exponent = jnp.exp(logits)
    total_part = jnp.sum(exponent, axis=1)
    target_part = jnp.sum(jnp.where(matches, logits, jnp.float32(0.0)), axis=1)
    weights = lax.optimization_barrier(exponent.astype(jnp.bfloat16))
    unscaled = jnp.dot(weights, both_centers, preferred_element_type=jnp.float32)
    own_center = jnp.dot(matches.astype(jnp.bfloat16), both_centers, preferred_element_type=jnp.float32)

    h = batch_count // 2

    def to_dest(values):
        tail = values.shape[1:]
        values = values.reshape((2, h, class_count, rows_here) + tail)
        values = jnp.moveaxis(values, 2, 0)
        values = jnp.swapaxes(values, 1, 2)
        return values.reshape((class_count, batch_count, rows_here) + tail)

    def pad(values):
        return jnp.pad(values, [(0, 0)] * (values.ndim - 1) + [(0, EXTRA - values.shape[-1])])

    block_rows = jnp.broadcast_to(
        jnp.stack([pad(total_part.reshape(batch_count, half)), pad(target_part.reshape(batch_count, half))], axis=1)[None],
        (class_count, batch_count, 2, EXTRA),
    )
    own_totals = pad(to_dest(total_part))[:, :, None, :]
    extra = jnp.concatenate(
        [block_rows, own_totals, jnp.zeros((class_count, batch_count, rows_here - 3, EXTRA), jnp.float32)], axis=2
    )
    unscaled, own_center, extra = to_dest(unscaled), to_dest(own_center), extra
    for axis in ("cls", "dp"):
        unscaled, own_center, extra = reduce_stage(unscaled, own_center, extra, axis)
    summed = jnp.concatenate([unscaled, own_center, extra], axis=-1)

    half_total = summed[0, 2 * width : 2 * width + half]
    half_target = summed[1, 2 * width : 2 * width + half]
    other_total, other_target = lax.ppermute((half_total, half_target), "section", swap)
    first = section == 0
    block_total = jnp.where(first, jnp.concatenate([half_total, other_total]), jnp.concatenate([other_total, half_total]))
    block_target = jnp.where(first, jnp.concatenate([half_target, other_target]), jnp.concatenate([other_target, half_target]))
    row_loss = jnp.log(block_total) - block_target

    unscaled_rows = summed[:, :width]
    own_rows = summed[:, width : 2 * width]
    totals_here = summed[2, 2 * width : 2 * width + rows_here]
    unit_grad = LOGIT_SCALE * (unscaled_rows / totals_here[:, None] - own_rows)
    source_batch = (batch % 2) * h + batch // 2
    offset = source_batch * half + cls * rows_here
    emb_rows = lax.dynamic_slice_in_dim(emb_float, offset, rows_here, 0)
    norm_rows = lax.dynamic_slice_in_dim(row_norm, offset, rows_here, 0)
    unit_float = emb_rows / norm_rows[:, None]
    along = jnp.sum(unit_float * unit_grad, axis=1, keepdims=True)
    computed = (unit_grad - unit_float * along) / norm_rows[:, None]

    pairs = [
        (s * batch_count + e, (1 - s) * batch_count + (e ^ 1))
        for s in range(2)
        for e in range(batch_count)
        if e % 2 != s
    ]
    received = lax.ppermute(computed, ("section", "dp"), pairs)
    feature_grad = jnp.where(batch % 2 == section, computed, received)
    return (feature_grad, row_loss)


def solution(mesh):
    return jax.shard_map(
        on_device,
        mesh=mesh,
        in_specs=(
            P("dp", None),
            P(("section", "dp", "cls"), None),
            P(("section", "dp", "cls"), None),
            P("dp"),
        ),
        out_specs=(P(("section", "dp", "cls"), None), P("dp")),
        check_vma=False,
    )
```

```python
import jax
import jax.numpy as jnp
from jax import lax
from jax.sharding import PartitionSpec as P

LOGIT_SCALE = 64.0
MARGIN = 0.35
EPSILON = 1e-06
EXTRA = 128


def split_pair(values):
    high = lax.reduce_precision(values, exponent_bits=8, mantissa_bits=7)
    low = (values - high).astype(jnp.bfloat16)
    return high.astype(jnp.bfloat16), low


def reduce_stage(unscaled, own_center, extra, axis):
    width, rows = unscaled.shape[-1], extra.shape[-2]
    unscaled_high, unscaled_low = split_pair(unscaled)
    extra_high, extra_low = split_pair(extra[..., :3, :])
    spare = jnp.zeros(extra.shape[:-2] + (rows - 6, extra.shape[-1]), jnp.bfloat16)
    extra_packed = jnp.concatenate([extra_high, extra_low, spare], axis=-2)
    packed = jnp.concatenate(
        [unscaled_high, unscaled_low, own_center.astype(jnp.bfloat16), extra_packed], axis=-1
    )
    packed = lax.all_to_all(packed, axis, 0, 0, tiled=False).astype(jnp.float32)
    unscaled = (packed[..., :width] + packed[..., width : 2 * width]).sum(0)
    own_center = packed[..., 2 * width : 3 * width].sum(0)
    extra_sum = (packed[..., 3 * width :][..., :3, :] + packed[..., 3 * width :][..., 3:6, :]).sum(0)
    extra = jnp.concatenate([extra_sum, jnp.zeros(extra_sum.shape[:-2] + (rows - 3, extra_sum.shape[-1]), jnp.float32)], axis=-2)
    return unscaled, own_center, extra


def on_device(embeddings, centers, sample_ids, labels):
    section_count = lax.axis_size("section")
    batch_count = lax.axis_size("dp")
    class_count = lax.axis_size("cls")
    assert section_count == 2 and batch_count % 2 == 0
    section = lax.axis_index("section")
    batch = lax.axis_index("dp")
    cls = lax.axis_index("cls")
    shard_index = lax.axis_index(("section", "dp", "cls"))
    swap = [(0, 1), (1, 0)]
    per_shard = centers.shape[0]
    width = embeddings.shape[1]
    rows_per_batch = embeddings.shape[0]
    half = rows_per_batch // section_count
    devices = section_count * batch_count * class_count
    rows_here = rows_per_batch * batch_count // devices
    assert half == class_count * rows_here and rows_here >= 6 and half <= EXTRA and rows_here <= EXTRA

    my_rows = lax.dynamic_slice_in_dim(embeddings, section * half, half, 0)
    my_labels = lax.dynamic_slice_in_dim(labels, section * half, half, 0)
    pieces = jnp.stack([my_labels % 256, (my_labels // 256) % 256, my_labels // 65536], axis=1)
    packed = jnp.concatenate(
        [my_rows, pieces.astype(jnp.bfloat16), jnp.zeros((half, EXTRA - 3), jnp.bfloat16)], axis=1
    )
    packed = lax.all_to_all(
        jnp.broadcast_to(packed[None], (batch_count,) + packed.shape), "dp", 0, 0, tiled=False
    ).reshape(batch_count * half, width + EXTRA)
    gathered = packed[:, :width]
    received = packed[:, width : width + 3].astype(jnp.int32)
    label_all = received[:, 0] + 256 * received[:, 1] + 65536 * received[:, 2]

    local_ids = sample_ids[0]
    chosen = jnp.take(centers, local_ids, axis=0).astype(jnp.float32)
    center_norm = jnp.sqrt(jnp.sum(chosen * chosen, axis=1) + EPSILON)
    unit_centers = (chosen / center_norm[:, None]).astype(jnp.bfloat16)
    global_ids = local_ids + shard_index * per_shard
    partner_centers = lax.ppermute(unit_centers, "section", swap)
    partner_ids = lax.ppermute(global_ids, "section", swap)
    both_centers = jnp.concatenate([unit_centers, partner_centers], axis=0)
    both_ids = jnp.concatenate([global_ids, partner_ids], axis=0)

    emb_float = gathered.astype(jnp.float32)
    row_norm = jnp.sqrt(jnp.sum(emb_float * emb_float, axis=1) + EPSILON)
    unit_rows = (emb_float / row_norm[:, None]).astype(jnp.bfloat16)
    cosine = lax.dot_general(
        unit_rows, both_centers, (((1,), (1,)), ((), ())), preferred_element_type=jnp.float32
    )
    matches = both_ids[None, :] == label_all[:, None]
    logits = LOGIT_SCALE * cosine - LOGIT_SCALE * MARGIN * matches.astype(jnp.float32)
    exponent = jnp.exp(logits)
    total_part = jnp.sum(exponent, axis=1)
    target_part = jnp.sum(jnp.where(matches, logits, jnp.float32(0.0)), axis=1)
    weights = lax.optimization_barrier(exponent.astype(jnp.bfloat16))
    unscaled = jnp.dot(weights, both_centers, preferred_element_type=jnp.float32)
    column_ids = jnp.arange(both_ids.shape[0], dtype=jnp.int32)
    position = jnp.sum(jnp.where(matches, column_ids[None, :], 0), axis=1)
    owned = jnp.any(matches, axis=1)
    own_center = jnp.where(owned[:, None], jnp.take(both_centers, position, axis=0), jnp.bfloat16(0)).astype(jnp.float32)

    h = batch_count // 2

    def to_dest(values):
        tail = values.shape[1:]
        values = values.reshape((2, h, class_count, rows_here) + tail)
        values = jnp.moveaxis(values, 2, 0)
        values = jnp.swapaxes(values, 1, 2)
        return values.reshape((class_count, batch_count, rows_here) + tail)

    def pad(values):
        return jnp.pad(values, [(0, 0)] * (values.ndim - 1) + [(0, EXTRA - values.shape[-1])])

    block_rows = jnp.broadcast_to(
        jnp.stack([pad(total_part.reshape(batch_count, half)), pad(target_part.reshape(batch_count, half))], axis=1)[None],
        (class_count, batch_count, 2, EXTRA),
    )
    own_totals = pad(to_dest(total_part))[:, :, None, :]
    extra = jnp.concatenate(
        [block_rows, own_totals, jnp.zeros((class_count, batch_count, rows_here - 3, EXTRA), jnp.float32)], axis=2
    )
    unscaled, own_center, extra = to_dest(unscaled), to_dest(own_center), extra
    for axis in ("cls", "dp"):
        unscaled, own_center, extra = reduce_stage(unscaled, own_center, extra, axis)
    summed = jnp.concatenate([unscaled, own_center, extra], axis=-1)

    half_total = summed[0, 2 * width : 2 * width + half]
    half_target = summed[1, 2 * width : 2 * width + half]
    other_total, other_target = lax.ppermute((half_total, half_target), "section", swap)
    first = section == 0
    block_total = jnp.where(first, jnp.concatenate([half_total, other_total]), jnp.concatenate([other_total, half_total]))
    block_target = jnp.where(first, jnp.concatenate([half_target, other_target]), jnp.concatenate([other_target, half_target]))
    row_loss = jnp.log(block_total) - block_target

    unscaled_rows = summed[:, :width]
    own_rows = summed[:, width : 2 * width]
    totals_here = summed[2, 2 * width : 2 * width + rows_here]
    unit_grad = LOGIT_SCALE * (unscaled_rows / totals_here[:, None] - own_rows)
    source_batch = (batch % 2) * h + batch // 2
    offset = source_batch * half + cls * rows_here
    emb_rows = lax.dynamic_slice_in_dim(emb_float, offset, rows_here, 0)
    norm_rows = lax.dynamic_slice_in_dim(row_norm, offset, rows_here, 0)
    unit_float = emb_rows / norm_rows[:, None]
    along = jnp.sum(unit_float * unit_grad, axis=1, keepdims=True)
    computed = (unit_grad - unit_float * along) / norm_rows[:, None]

    pairs = [
        (s * batch_count + e, (1 - s) * batch_count + (e ^ 1))
        for s in range(2)
        for e in range(batch_count)
        if e % 2 != s
    ]
    received = lax.ppermute(computed, ("section", "dp"), pairs)
    feature_grad = jnp.where(batch % 2 == section, computed, received)
    return (feature_grad, row_loss)


def solution(mesh):
    return jax.shard_map(
        on_device,
        mesh=mesh,
        in_specs=(
            P("dp", None),
            P(("section", "dp", "cls"), None),
            P(("section", "dp", "cls"), None),
            P("dp"),
        ),
        out_specs=(P(("section", "dp", "cls"), None), P("dp")),
        check_vma=False,
    )
```

```python
import jax
import jax.numpy as jnp
from jax import lax
from jax.sharding import PartitionSpec as P

LOGIT_SCALE = 64.0
MARGIN = 0.35
EPSILON = 1e-06
EXTRA = 128


def split_pair(values):
    high = lax.reduce_precision(values, exponent_bits=8, mantissa_bits=7)
    low = (values - high).astype(jnp.bfloat16)
    return high.astype(jnp.bfloat16), low


def reduce_stage(unscaled, own_center, extra, axis):
    width, rows = unscaled.shape[-1], extra.shape[-2]
    unscaled_high, unscaled_low = split_pair(unscaled)
    extra_high, extra_low = split_pair(extra[..., :3, :])
    spare = jnp.zeros(extra.shape[:-2] + (rows - 6, extra.shape[-1]), jnp.bfloat16)
    extra_packed = jnp.concatenate([extra_high, extra_low, spare], axis=-2)
    packed = jnp.concatenate(
        [unscaled_high, unscaled_low, own_center.astype(jnp.bfloat16), extra_packed], axis=-1
    )
    packed = lax.all_to_all(packed, axis, 0, 0, tiled=False)

    def total(part):
        return jnp.sum(part, axis=0, dtype=jnp.float32)

    unscaled = total(packed[..., :width]) + total(packed[..., width : 2 * width])
    own_center = total(packed[..., 2 * width : 3 * width])
    extra_sum = total(packed[..., 3 * width :][..., :3, :]) + total(packed[..., 3 * width :][..., 3:6, :])
    extra = jnp.concatenate([extra_sum, jnp.zeros(extra_sum.shape[:-2] + (rows - 3, extra_sum.shape[-1]), jnp.float32)], axis=-2)
    return unscaled, own_center, extra


def on_device(embeddings, centers, sample_ids, labels):
    section_count = lax.axis_size("section")
    batch_count = lax.axis_size("dp")
    class_count = lax.axis_size("cls")
    assert section_count == 2 and batch_count % 2 == 0
    section = lax.axis_index("section")
    batch = lax.axis_index("dp")
    cls = lax.axis_index("cls")
    shard_index = lax.axis_index(("section", "dp", "cls"))
    swap = [(0, 1), (1, 0)]
    per_shard = centers.shape[0]
    width = embeddings.shape[1]
    rows_per_batch = embeddings.shape[0]
    half = rows_per_batch // section_count
    devices = section_count * batch_count * class_count
    rows_here = rows_per_batch * batch_count // devices
    assert half == class_count * rows_here and rows_here >= 6 and half <= EXTRA and rows_here <= EXTRA

    my_rows = lax.dynamic_slice_in_dim(embeddings, section * half, half, 0)
    my_labels = lax.dynamic_slice_in_dim(labels, section * half, half, 0)
    pieces = jnp.stack([my_labels % 256, (my_labels // 256) % 256, my_labels // 65536], axis=1)
    packed = jnp.concatenate(
        [my_rows, pieces.astype(jnp.bfloat16), jnp.zeros((half, EXTRA - 3), jnp.bfloat16)], axis=1
    )
    packed = lax.all_to_all(
        jnp.broadcast_to(packed[None], (batch_count,) + packed.shape), "dp", 0, 0, tiled=False
    ).reshape(batch_count * half, width + EXTRA)
    gathered = packed[:, :width]
    received = packed[:, width : width + 3].astype(jnp.int32)
    label_all = received[:, 0] + 256 * received[:, 1] + 65536 * received[:, 2]

    local_ids = sample_ids[0]
    chosen = jnp.take(centers, local_ids, axis=0).astype(jnp.float32)
    center_norm = jnp.sqrt(jnp.sum(chosen * chosen, axis=1) + EPSILON)
    unit_centers = (chosen / center_norm[:, None]).astype(jnp.bfloat16)
    global_ids = local_ids + shard_index * per_shard
    partner_centers = lax.ppermute(unit_centers, "section", swap)
    partner_ids = lax.ppermute(global_ids, "section", swap)
    both_centers = jnp.concatenate([unit_centers, partner_centers], axis=0)
    both_ids = jnp.concatenate([global_ids, partner_ids], axis=0)

    emb_float = gathered.astype(jnp.float32)
    row_norm = jnp.sqrt(jnp.sum(emb_float * emb_float, axis=1) + EPSILON)
    unit_rows = (emb_float / row_norm[:, None]).astype(jnp.bfloat16)
    cosine = lax.dot_general(
        unit_rows, both_centers, (((1,), (1,)), ((), ())), preferred_element_type=jnp.float32
    )
    matches = both_ids[None, :] == label_all[:, None]
    logits = LOGIT_SCALE * cosine - LOGIT_SCALE * MARGIN * matches.astype(jnp.float32)
    exponent = jnp.exp(logits)
    total_part = jnp.sum(exponent, axis=1)
    target_part = jnp.sum(jnp.where(matches, logits, jnp.float32(0.0)), axis=1)
    weights = lax.optimization_barrier(exponent.astype(jnp.bfloat16))
    unscaled = jnp.dot(weights, both_centers, preferred_element_type=jnp.float32)
    own_center = jnp.dot(matches.astype(jnp.bfloat16), both_centers, preferred_element_type=jnp.float32)

    h = batch_count // 2

    def to_dest(values):
        tail = values.shape[1:]
        values = values.reshape((2, h, class_count, rows_here) + tail)
        values = jnp.moveaxis(values, 2, 0)
        values = jnp.swapaxes(values, 1, 2)
        return values.reshape((class_count, batch_count, rows_here) + tail)

    def pad(values):
        return jnp.pad(values, [(0, 0)] * (values.ndim - 1) + [(0, EXTRA - values.shape[-1])])

    block_rows = jnp.broadcast_to(
        jnp.stack([pad(total_part.reshape(batch_count, half)), pad(target_part.reshape(batch_count, half))], axis=1)[None],
        (class_count, batch_count, 2, EXTRA),
    )
    own_totals = pad(to_dest(total_part))[:, :, None, :]
    extra = jnp.concatenate(
        [block_rows, own_totals, jnp.zeros((class_count, batch_count, rows_here - 3, EXTRA), jnp.float32)], axis=2
    )
    unscaled, own_center, extra = to_dest(unscaled), to_dest(own_center), extra
    for axis in ("cls", "dp"):
        unscaled, own_center, extra = reduce_stage(unscaled, own_center, extra, axis)
    summed = jnp.concatenate([unscaled, own_center, extra], axis=-1)

    half_total = summed[0, 2 * width : 2 * width + half]
    half_target = summed[1, 2 * width : 2 * width + half]
    other_total, other_target = lax.ppermute((half_total, half_target), "section", swap)
    first = section == 0
    block_total = jnp.where(first, jnp.concatenate([half_total, other_total]), jnp.concatenate([other_total, half_total]))
    block_target = jnp.where(first, jnp.concatenate([half_target, other_target]), jnp.concatenate([other_target, half_target]))
    row_loss = jnp.log(block_total) - block_target

    unscaled_rows = summed[:, :width]
    own_rows = summed[:, width : 2 * width]
    totals_here = summed[2, 2 * width : 2 * width + rows_here]
    unit_grad = LOGIT_SCALE * (unscaled_rows / totals_here[:, None] - own_rows)
    source_batch = (batch % 2) * h + batch // 2
    offset = source_batch * half + cls * rows_here
    emb_rows = lax.dynamic_slice_in_dim(emb_float, offset, rows_here, 0)
    norm_rows = lax.dynamic_slice_in_dim(row_norm, offset, rows_here, 0)
    unit_float = emb_rows / norm_rows[:, None]
    along = jnp.sum(unit_float * unit_grad, axis=1, keepdims=True)
    computed = (unit_grad - unit_float * along) / norm_rows[:, None]

    pairs = [
        (s * batch_count + e, (1 - s) * batch_count + (e ^ 1))
        for s in range(2)
        for e in range(batch_count)
        if e % 2 != s
    ]
    received = lax.ppermute(computed, ("section", "dp"), pairs)
    feature_grad = jnp.where(batch % 2 == section, computed, received)
    return (feature_grad, row_loss)


def solution(mesh):
    return jax.shard_map(
        on_device,
        mesh=mesh,
        in_specs=(
            P("dp", None),
            P(("section", "dp", "cls"), None),
            P(("section", "dp", "cls"), None),
            P("dp"),
        ),
        out_specs=(P(("section", "dp", "cls"), None), P("dp")),
        check_vma=False,
    )
```

```python
import jax
import jax.numpy as jnp
from jax import lax
from jax.sharding import PartitionSpec as P

LOGIT_SCALE = 64.0
MARGIN = 0.35
EPSILON = 1e-06
EXTRA = 128


def split_pair(values):
    high = lax.reduce_precision(values, exponent_bits=8, mantissa_bits=7)
    low = (values - high).astype(jnp.bfloat16)
    return high.astype(jnp.bfloat16), low


def reduce_stage(unscaled, own_center, extra, axis):
    width, rows = unscaled.shape[-1], extra.shape[-2]
    unscaled_high, unscaled_low = split_pair(unscaled)
    extra_high, extra_low = split_pair(extra[..., :3, :])
    spare = jnp.zeros(extra.shape[:-2] + (rows - 6, extra.shape[-1]), jnp.bfloat16)
    extra_packed = jnp.concatenate([extra_high, extra_low, spare], axis=-2)
    packed = jnp.concatenate(
        [unscaled_high, unscaled_low, own_center.astype(jnp.bfloat16), extra_packed], axis=-1
    )
    packed = lax.all_to_all(packed, axis, 0, 0, tiled=False).astype(jnp.float32)
    unscaled = (packed[..., :width] + packed[..., width : 2 * width]).sum(0)
    own_center = packed[..., 2 * width : 3 * width].sum(0)
    extra_sum = (packed[..., 3 * width :][..., :3, :] + packed[..., 3 * width :][..., 3:6, :]).sum(0)
    extra = jnp.concatenate([extra_sum, jnp.zeros(extra_sum.shape[:-2] + (rows - 3, extra_sum.shape[-1]), jnp.float32)], axis=-2)
    return unscaled, own_center, extra


def on_device(embeddings, centers, sample_ids, labels):
    section_count = lax.axis_size("section")
    batch_count = lax.axis_size("dp")
    class_count = lax.axis_size("cls")
    assert section_count == 2 and batch_count % 2 == 0
    section = lax.axis_index("section")
    batch = lax.axis_index("dp")
    cls = lax.axis_index("cls")
    shard_index = lax.axis_index(("section", "dp", "cls"))
    swap = [(0, 1), (1, 0)]
    per_shard = centers.shape[0]
    width = embeddings.shape[1]
    rows_per_batch = embeddings.shape[0]
    half = rows_per_batch // section_count
    devices = section_count * batch_count * class_count
    rows_here = rows_per_batch * batch_count // devices
    assert half == class_count * rows_here and rows_here >= 6 and half <= EXTRA and rows_here <= EXTRA

    my_rows = lax.dynamic_slice_in_dim(embeddings, section * half, half, 0)
    my_labels = lax.dynamic_slice_in_dim(labels, section * half, half, 0)
    pieces = jnp.stack([my_labels % 256, (my_labels // 256) % 256, my_labels // 65536], axis=1)
    packed = jnp.concatenate(
        [my_rows, pieces.astype(jnp.bfloat16), jnp.zeros((half, EXTRA - 3), jnp.bfloat16)], axis=1
    )
    packed = lax.all_to_all(
        jnp.broadcast_to(packed[None], (batch_count,) + packed.shape), "dp", 0, 0, tiled=False
    ).reshape(batch_count * half, width + EXTRA)
    gathered = packed[:, :width]
    received = packed[:, width : width + 3].astype(jnp.int32)
    label_all = received[:, 0] + 256 * received[:, 1] + 65536 * received[:, 2]

    local_ids = sample_ids[0]
    chosen = jnp.take(centers, local_ids, axis=0).astype(jnp.float32)
    center_norm = jnp.sqrt(jnp.sum(chosen * chosen, axis=1) + EPSILON)
    unit_centers = (chosen / center_norm[:, None]).astype(jnp.bfloat16)
    global_ids = local_ids + shard_index * per_shard
    partner_centers = lax.ppermute(unit_centers, "section", swap)
    partner_ids = lax.ppermute(global_ids, "section", swap)
    both_centers = jnp.concatenate([unit_centers, partner_centers], axis=0)
    both_ids = jnp.concatenate([global_ids, partner_ids], axis=0)

    emb_float = gathered.astype(jnp.float32)
    row_norm = jnp.sqrt(jnp.sum(emb_float * emb_float, axis=1) + EPSILON)
    unit_rows = (emb_float / row_norm[:, None]).astype(jnp.bfloat16)
    cosine = lax.dot_general(
        unit_rows, both_centers, (((1,), (1,)), ((), ())), preferred_element_type=jnp.float32
    )
    matches = both_ids[None, :] == label_all[:, None]
    logits = LOGIT_SCALE * cosine - LOGIT_SCALE * MARGIN * matches.astype(jnp.float32)
    exponent = jnp.exp(logits)
    total_part = jnp.sum(exponent, axis=1)
    target_part = jnp.sum(jnp.where(matches, logits, jnp.float32(0.0)), axis=1)
    weights = lax.optimization_barrier(exponent.astype(jnp.bfloat16))
    unscaled = jnp.dot(weights, both_centers, preferred_element_type=jnp.float32)
    own_center = jnp.dot(matches.astype(jnp.bfloat16), both_centers, preferred_element_type=jnp.float32)

    h = batch_count // 2

    def to_dest(values):
        tail = values.shape[1:]
        values = values.reshape((2, h, class_count, rows_here) + tail)
        values = jnp.moveaxis(values, 2, 0)
        values = jnp.swapaxes(values, 1, 2)
        return values.reshape((class_count, batch_count, rows_here) + tail)

    def pad(values):
        return jnp.pad(values, [(0, 0)] * (values.ndim - 1) + [(0, EXTRA - values.shape[-1])])

    block_rows = jnp.broadcast_to(
        jnp.stack([pad(total_part.reshape(batch_count, half)), pad(target_part.reshape(batch_count, half))], axis=1)[None],
        (class_count, batch_count, 2, EXTRA),
    )
    own_totals = pad(to_dest(total_part))[:, :, None, :]
    extra = jnp.concatenate(
        [block_rows, own_totals, jnp.zeros((class_count, batch_count, rows_here - 3, EXTRA), jnp.float32)], axis=2
    )
    unscaled, own_center, extra = to_dest(unscaled), to_dest(own_center), extra
    for axis in ("cls", "dp"):
        unscaled, own_center, extra = reduce_stage(unscaled, own_center, extra, axis)
    summed = jnp.concatenate([unscaled, own_center, extra], axis=-1)

    half_total = summed[0, 2 * width : 2 * width + half]
    half_target = summed[1, 2 * width : 2 * width + half]
    other_total, other_target = lax.ppermute(jnp.stack([half_total, half_target]), "section", swap)
    first = section == 0
    block_total = jnp.where(first, jnp.concatenate([half_total, other_total]), jnp.concatenate([other_total, half_total]))
    block_target = jnp.where(first, jnp.concatenate([half_target, other_target]), jnp.concatenate([other_target, half_target]))
    row_loss = jnp.log(block_total) - block_target

    unscaled_rows = summed[:, :width]
    own_rows = summed[:, width : 2 * width]
    totals_here = summed[2, 2 * width : 2 * width + rows_here]
    unit_grad = LOGIT_SCALE * (unscaled_rows / totals_here[:, None] - own_rows)
    source_batch = (batch % 2) * h + batch // 2
    offset = source_batch * half + cls * rows_here
    emb_rows = lax.dynamic_slice_in_dim(emb_float, offset, rows_here, 0)
    norm_rows = lax.dynamic_slice_in_dim(row_norm, offset, rows_here, 0)
    unit_float = emb_rows / norm_rows[:, None]
    along = jnp.sum(unit_float * unit_grad, axis=1, keepdims=True)
    computed = (unit_grad - unit_float * along) / norm_rows[:, None]

    pairs = [
        (s * batch_count + e, (1 - s) * batch_count + (e ^ 1))
        for s in range(2)
        for e in range(batch_count)
        if e % 2 != s
    ]
    received = lax.ppermute(computed, ("section", "dp"), pairs)
    feature_grad = jnp.where(batch % 2 == section, computed, received)
    return (feature_grad, row_loss)


def solution(mesh):
    return jax.shard_map(
        on_device,
        mesh=mesh,
        in_specs=(
            P("dp", None),
            P(("section", "dp", "cls"), None),
            P(("section", "dp", "cls"), None),
            P("dp"),
        ),
        out_specs=(P(("section", "dp", "cls"), None), P("dp")),
        check_vma=False,
    )
```
